32 devices in a mesh: groups: 2 (over y), queue: 4 (over z), dp: 4 (over x, core).
Axes of the slice: x: 2, y: 2, z: 4, core: 2. Of those that a mesh axis runs over, the one named last changes fastest.
Arguments:
- query_inputs: bfloat16 [8192, 1024], P(('groups', 'queue', 'dp')), parts along dimension 0, may hold values from -30 to 30
- key_inputs: bfloat16 [512, 1024], P(('groups', 'queue', 'dp')), parts along dimension 0, may hold values from -6 to 6
- query_weight: bfloat16 [1024, 1024], replicated, may hold values from -4 to 4
- key_weight: bfloat16 [1024, 1024], replicated, may hold values from -0.1875 to 0.1875
- queue_keys: bfloat16 [2048, 1024], P(('groups', 'queue')), parts along dimension 0, may hold values from -2 to 2
- write_pointer: int32 [2], P('groups'), parts along dimension 0, may hold values from 0 to 255
- slot_owner: int32 [32], P('groups'), parts along dimension 0, may hold values from 0 to 15, each once
- positive_index: int32 [8192], P(('groups', 'queue', 'dp')), parts along dimension 0, may hold values from 0 to 1023
Outputs:
- loss: float32 [8192], P(('groups', 'queue', 'dp')), parts along dimension 0
- query_weight_grad: float32 [2048, 1024], P(('groups', 'queue', 'dp')), parts along dimension 0
- new_queue: bfloat16 [2048, 1024], P(('groups', 'queue')), parts along dimension 0
The draws below stay inside these ranges and needn't reach their ends.
There are 2 independent parts, one for each index of `groups`. The reference program is written for one: setup_inputs(seed, part) draws one part's arguments, and reference() takes and returns one part's arrays. A program takes and returns all parts, laid end to end along the dimension named above; an argument that names none is the same for every part. Nothing has to cross between parts.
Inputs may be any that keep to these rules, and one draw needn't show every extreme that they name: slot_owner is a permutation of 0 to 15.
All inputs are finite; a program needn't handle non-finite values.
Results may differ from the reference program's by a relative error of at most 0.0075.
Values may be sent and summed in bfloat16 or wider, within the bound.
No kernel may reach another device: no remote copies, remote signals or barrier semaphores. Data moves between devices by JAX's collectives and lax.ppermute only.
A program may use at most 192 MiB of HBM per device.

```python
import math
import jax
import jax.numpy as jnp
from jax import lax

D = 1024
Q_DEV = 256
K_DEV = 256
NEW_DEV = 16
QUERIES = 4096
KEYS = 1024
BLOCKS = 16
NEWKEYS = 256
N_QUEUE = 4
N_DP = 4


def draw_queue_keys(key, part):
    key_entries = jax.random.fold_in(key, 11)
    spread = D ** (-0.5)
    entries = jnp.clip(jax.random.normal(key_entries, (KEYS, D), jnp.float32), -6.0, 6.0) * spread
    return entries.astype(jnp.bfloat16)


def draw_query_inputs(key, part):
    key_entries = jax.random.fold_in(key, 13)
    group_count = N_QUEUE * N_DP
    pairing = jax.random.permutation(jax.random.fold_in(key, 17), group_count)
    row_index = jnp.arange(QUERIES, dtype=jnp.int32)
    column_index = jnp.arange(D, dtype=jnp.int32)
    column_block = column_index // (D // group_count)
    row_pair = pairing[row_index // Q_DEV]
    spike_gain = jnp.where(row_pair[:, None] == column_block[None, :], 4.0, 1.0)
    entries = jnp.clip(jax.random.normal(key_entries, (QUERIES, D), jnp.float32), -6.0, 6.0) * spike_gain
    return entries.astype(jnp.bfloat16)


def draw_query_weight(key, part):
    key_entries = jax.random.fold_in(key, 19)
    spread = D ** (-0.5)
    entries = jnp.clip(jax.random.normal(key_entries, (D, D), jnp.float32), -6.0, 6.0) * spread
    return entries.astype(jnp.bfloat16)


def with_ends(result, rng, low, high):
    place = [jax.random.randint(jax.random.fold_in(rng, axis), (), 0, length) for axis, length in enumerate(result.shape)]
    longest = result.shape.index(max(result.shape))
    neighbour = place[:longest] + [(place[longest] + 1) % result.shape[longest]] + place[longest + 1:]
    return result.at[tuple(place)].set(low).at[tuple(neighbour)].set(high)


def level_of(rng, shape, shards, smallest, top_value):
    loudness = 1.0
    for dim, parts in shards:
        heights = jax.random.uniform(jax.random.fold_in(jax.random.fold_in(rng, 6), dim), (parts,), jnp.float32, smallest / len(shards), top_value / len(shards))
        loudness = loudness * jnp.repeat(jnp.exp(heights), shape[dim] // parts).reshape((-1,) + (1,) * (len(shape) - 1 - dim))
    return loudness


def normal_values(rng, extent, scale, bound, pieces=(), kind=jnp.bfloat16):
    level = level_of(rng, extent, pieces, -0.22, 0.18) if pieces else 1.0
    result = jax.random.normal(rng, extent, jnp.float32) * scale * level
    return jnp.minimum(jnp.maximum(result, -bound), bound).astype(kind)


def setup_inputs(seed: int = 0, part: int = 0) -> dict:
    key_list = jax.random.split(jax.random.key(seed), 9)
    part_keys = jax.random.split(jax.random.fold_in(key_list[8], part), 9)
    return {
        "query_inputs": draw_query_inputs(jax.random.fold_in(jax.random.fold_in(key_list[8], part), 71), part),
        "key_inputs": normal_values(part_keys[1], (NEWKEYS, D), 1.0, 6.0, ((0, 16),)),
        "query_weight": draw_query_weight(jax.random.fold_in(key_list[8], 71), part),
        "key_weight": normal_values(key_list[3], (D, D), D ** -0.5, 0.1875),
        "queue_keys": draw_queue_keys(jax.random.fold_in(jax.random.fold_in(key_list[8], part), 71), part),
        "write_pointer": jax.random.randint(part_keys[5], (1,), 0, K_DEV).astype(jnp.int32),
        "slot_owner": jax.random.permutation(part_keys[6], BLOCKS).astype(jnp.int32),
        "positive_index": with_ends(jax.random.randint(part_keys[7], (QUERIES,), 0, KEYS), jax.random.fold_in(part_keys[7], 1), 0, KEYS - 1).astype(jnp.int32),
    }


temper = 0.05

def unit_rows(matrix):
    return matrix * lax.rsqrt(lax.optimization_barrier(jnp.sum(matrix * matrix, -1, keepdims=True)) + 1e-06)

def reference(query_inputs, key_inputs, query_weight, key_weight, queue_keys, write_pointer, slot_owner, positive_index):
    query = jnp.dot(query_inputs, query_weight, preferred_element_type=jnp.float32)
    inv_len = lax.rsqrt(lax.optimization_barrier(jnp.sum(query * query, -1, keepdims=True)) + 1e-06)
    unit_f = query * inv_len
    unit = unit_f.astype(jnp.bfloat16)
    width = math.gcd(QUERIES, 2048)

    def one_block(rows):
        scores = jnp.dot(rows, queue_keys.T, preferred_element_type=jnp.float32) / temper
        top = lax.optimization_barrier(jnp.max(scores, -1))
        expo = jnp.exp(scores - top[:, None])
        total = lax.optimization_barrier(jnp.sum(expo, -1))
        mixture = jnp.dot(expo.astype(jnp.bfloat16), queue_keys, preferred_element_type=jnp.float32) / total[:, None]
        return (top, total, mixture)
    top, total, mixture = lax.map(one_block, unit.reshape(QUERIES // width, width, D))
    top = top.reshape(QUERIES)
    total = total.reshape(QUERIES)
    mixture = mixture.reshape(QUERIES, D)
    chosen = jnp.take(queue_keys, positive_index, axis=0).astype(jnp.float32)
    positive = lax.optimization_barrier(jnp.sum(unit.astype(jnp.float32) * chosen, -1)) / temper
    loss = top + jnp.log(total) - positive
    grad_unit = (mixture - chosen) / temper
    grad_query = ((grad_unit - unit_f * lax.optimization_barrier(jnp.sum(unit_f * grad_unit, -1, keepdims=True))) * inv_len).astype(jnp.bfloat16)
    query_weight_grad = jnp.dot(query_inputs.T, grad_query, preferred_element_type=jnp.float32)
    fresh = unit_rows(jnp.dot(key_inputs, key_weight, preferred_element_type=jnp.float32)).astype(jnp.bfloat16)
    rows = jnp.arange(KEYS, dtype=jnp.int32)
    shard = rows // K_DEV
    offset = (rows % K_DEV - write_pointer[0]) % K_DEV
    live = offset < N_DP * NEW_DEV
    slot = shard * N_DP + jnp.minimum(offset // NEW_DEV, N_DP - 1)
    inverse = jnp.zeros((BLOCKS,), jnp.int32).at[slot_owner].set(jnp.arange(BLOCKS, dtype=jnp.int32))
    source = (jnp.take(inverse, slot) * NEW_DEV + offset % NEW_DEV).astype(jnp.int32)
    new_queue = jnp.where(live[:, None], jnp.take(fresh, source, axis=0), queue_keys)
    return (loss, query_weight_grad, new_queue)
```

```python
import jax
import jax.numpy as jnp
from jax import lax
from jax.sharding import PartitionSpec as P

temper = 0.05


def shift(x, axis, n, step):
    return lax.ppermute(x, axis, [(i, (i + step) % n) for i in range(n)])


def swap(x, axis, n, bit):
    return lax.ppermute(x, axis, [(i, i ^ bit) for i in range(n)])


def dp_bits(n_dp):
    bits = []
    b = n_dp // 2
    while b >= 1:
        bits.append(b)
        b //= 2
    return bits


def gather_queue(queue_keys, fresh, n_q, n_dp):
    q = lax.axis_index("queue")
    dp = lax.axis_index("dp")
    k_dev, width = queue_keys.shape
    piece_rows = k_dev // n_dp
    piece = lax.dynamic_slice_in_dim(queue_keys, dp * piece_rows, piece_rows, 0)
    got = [shift((piece, fresh), "queue", n_q, s) for s in range(1, n_q)]
    remote = jnp.stack([g[0] for g in got])
    blocks = jnp.stack([fresh] + [g[1] for g in got])
    for t, bit in enumerate(dp_bits(n_dp)):
        other_remote, other_blocks = swap((remote, blocks), "dp", n_dp, bit)
        remote = jnp.stack([remote, other_remote], axis=t)
        blocks = jnp.stack([blocks, other_blocks], axis=t)
    remote = remote.reshape(-1, width)
    blocks = blocks.reshape(n_dp * n_q, -1, width)
    return remote, blocks


def reduce_scatter_rows(term, n_q, n_dp):
    q = lax.axis_index("queue")
    dp = lax.axis_index("dp")
    rows, width = term.shape
    share = rows // (n_q * n_dp)
    bits = dp_bits(n_dp)
    t = term.reshape((n_q,) + (2,) * len(bits) + (share, width))
    for axis in reversed(range(len(bits))):
        bit = bits[axis]
        mine = (dp // bit) % 2
        keep = lax.dynamic_index_in_dim(t, mine, 1 + axis, keepdims=False)
        send = lax.dynamic_index_in_dim(t, 1 - mine, 1 + axis, keepdims=False)
        t = keep + swap(send, "dp", n_dp, bit)
    t = t.reshape(n_q, share, width)
    acc = lax.dynamic_index_in_dim(t, q, 0, keepdims=False)
    for s in range(1, n_q):
        part = lax.dynamic_index_in_dim(t, (q + s) % n_q, 0, keepdims=False)
        acc = acc + shift(part, "queue", n_q, s)
    return acc


def body(
    query_inputs,
    key_inputs,
    query_weight,
    key_weight,
    queue_keys,
    write_pointer,
    slot_owner,
    positive_index,
):
    q_dev, width = query_inputs.shape
    k_dev = queue_keys.shape[0]
    new_dev = key_inputs.shape[0]
    n_dp = lax.axis_size("dp")
    n_q = lax.axis_size("queue")
    q = lax.axis_index("queue")
    dp = lax.axis_index("dp")
    piece_rows = k_dev // n_dp

    fresh = jnp.dot(key_inputs, key_weight, preferred_element_type=jnp.float32)
    fresh = (fresh * lax.rsqrt(jnp.sum(fresh * fresh, -1, keepdims=True) + 1e-06)).astype(
        jnp.bfloat16
    )
    remote, blocks = gather_queue(queue_keys, fresh, n_q, n_dp)

    query = jnp.dot(query_inputs, query_weight, preferred_element_type=jnp.float32)
    inv_len = lax.rsqrt(jnp.sum(query * query, -1, keepdims=True) + 1e-06)
    unit_f = query * inv_len
    unit = unit_f.astype(jnp.bfloat16)

    keys = jnp.concatenate([queue_keys, remote], axis=0)
    scores = (
        lax.dot_general(unit, keys, (((1,), (1,)), ((), ())), preferred_element_type=jnp.float32)
        / temper
    )
    top = jnp.max(scores, -1)
    expo = jnp.exp(scores - top[:, None])
    total = jnp.sum(expo, -1)
    mixture = jnp.dot(expo.astype(jnp.bfloat16), keys, preferred_element_type=jnp.float32)

    j = positive_index
    q_src = j // k_dev
    within = j % k_dev
    e = dp ^ (within // piece_rows)
    s = (q - q_src) % n_q
    far = k_dev + (e * (n_q - 1) + (s - 1)) * piece_rows + within % piece_rows
    where_row = jnp.where(q_src == q, within, far)
    chosen = jnp.take(keys, where_row, axis=0).astype(jnp.float32)

    mixture = mixture / total[:, None]
    positive = jnp.sum(unit.astype(jnp.float32) * chosen, -1) / temper
    loss = top + jnp.log(total) - positive
    grad_unit = (mixture - chosen) / temper
    grad_query = (
        (grad_unit - unit_f * jnp.sum(unit_f * grad_unit, -1, keepdims=True)) * inv_len
    ).astype(jnp.bfloat16)
    term = lax.dot_general(
        query_inputs, grad_query, (((0,), (0,)), ((), ())), preferred_element_type=jnp.float32
    )
    grad_rows = reduce_scatter_rows(term, n_q, n_dp)

    n_blocks = slot_owner.shape[0]
    slots_here = q * n_dp + jnp.arange(n_dp, dtype=jnp.int32)
    match = slot_owner[None, :] == slots_here[:, None]
    owner_block = jnp.sum(jnp.where(match, jnp.arange(n_blocks, dtype=jnp.int32)[None, :], 0), -1)
    offset = (jnp.arange(k_dev, dtype=jnp.int32) - write_pointer[0]) % k_dev
    live = offset < n_dp * new_dev
    sub_block = jnp.minimum(offset // new_dev, n_dp - 1)
    b = jnp.take(owner_block, sub_block)
    b_e = dp ^ (b % n_dp)
    b_s = (q - b // n_dp) % n_q
    flat = blocks.reshape(-1, width)
    source = (b_e * n_q + b_s) * new_dev + offset % new_dev
    new_queue = jnp.where(live[:, None], jnp.take(flat, source, axis=0), queue_keys)
    return (loss, grad_rows, new_queue)


def solution(mesh):
    in_specs = (
        P(("groups", "queue", "dp"), None),
        P(("groups", "queue", "dp"), None),
        P(),
        P(),
        P(("groups", "queue"), None),
        P("groups"),
        P("groups"),
        P(("groups", "queue", "dp")),
    )
    out_specs = (
        P(("groups", "queue", "dp")),
        P(("groups", "queue", "dp"), None),
        P(("groups", "queue"), None),
    )
    return jax.shard_map(body, mesh=mesh, in_specs=in_specs, out_specs=out_specs, check_vma=False)
```

```python
import jax
import jax.numpy as jnp
from jax import lax
from jax.sharding import PartitionSpec as P

temper = 0.05


def shift(x, axis, n, step):
    return lax.ppermute(x, axis, [(i, (i + step) % n) for i in range(n)])


def swap(x, axis, n, bit):
    return lax.ppermute(x, axis, [(i, i ^ bit) for i in range(n)])


def dp_bits(n_dp):
    bits = []
    b = n_dp // 2
    while b >= 1:
        bits.append(b)
        b //= 2
    return bits


def gather_queue(queue_keys, fresh, n_q, n_dp):
    dp = lax.axis_index("dp")
    k_dev, width = queue_keys.shape
    piece_rows = k_dev // n_dp
    piece = lax.dynamic_slice_in_dim(queue_keys, dp * piece_rows, piece_rows, 0)
    packed = jnp.concatenate([piece, fresh], axis=0)
    got = [shift(packed, "queue", n_q, s) for s in range(1, n_q)]
    payload = jnp.concatenate(
        [g[:piece_rows] for g in got] + [fresh] + [g[piece_rows:] for g in got], axis=0
    )
    for t, bit in enumerate(dp_bits(n_dp)):
        payload = jnp.stack([payload, swap(payload, "dp", n_dp, bit)], axis=t)
    return payload.reshape(n_dp, -1, width)


def reduce_scatter_grad(query_inputs, grad_query, n_q, n_dp):
    q = lax.axis_index("queue")
    dp = lax.axis_index("dp")
    q_dev, rows = query_inputs.shape
    width = grad_query.shape[1]
    share = rows // (n_q * n_dp)
    bits = dp_bits(n_dp)
    hb = bits[0]
    side = dp // hb
    x4 = query_inputs.reshape(q_dev, n_q, 2, hb * share)
    mine = lax.dynamic_index_in_dim(x4, side, 2, keepdims=False)
    other = lax.dynamic_index_in_dim(x4, 1 - side, 2, keepdims=False)
    got_x, got_g = swap((other, grad_query), "dp", n_dp, hb)
    xs = jnp.concatenate([mine, got_x], axis=0).reshape(2 * q_dev, n_q * hb * share)
    gs = jnp.concatenate([grad_query, got_g], axis=0)
    term = lax.dot_general(xs, gs, (((0,), (0,)), ((), ())), preferred_element_type=jnp.float32)
    rest = bits[1:]
    t = term.reshape((n_q,) + (2,) * len(rest) + (share, width))
    for axis in reversed(range(len(rest))):
        bit = rest[axis]
        me = (dp // bit) % 2
        keep = lax.dynamic_index_in_dim(t, me, 1 + axis, keepdims=False)
        send = lax.dynamic_index_in_dim(t, 1 - me, 1 + axis, keepdims=False)
        t = keep + swap(send, "dp", n_dp, bit)
    t = t.reshape(n_q, share, width)
    acc = lax.dynamic_index_in_dim(t, q, 0, keepdims=False)
    for s in range(1, n_q):
        part = lax.dynamic_index_in_dim(t, (q + s) % n_q, 0, keepdims=False)
        acc = acc + shift(part, "queue", n_q, s)
    return acc


def body(
    query_inputs,
    key_inputs,
    query_weight,
    key_weight,
    queue_keys,
    write_pointer,
    slot_owner,
    positive_index,
):
    q_dev, width = query_inputs.shape
    k_dev = queue_keys.shape[0]
    new_dev = key_inputs.shape[0]
    n_dp = lax.axis_size("dp")
    n_q = lax.axis_size("queue")
    q = lax.axis_index("queue")
    dp = lax.axis_index("dp")
    piece_rows = k_dev // n_dp
    far_rows = (n_q - 1) * piece_rows

    fresh = jnp.dot(key_inputs, key_weight, preferred_element_type=jnp.float32)
    fresh = (fresh * lax.rsqrt(jnp.sum(fresh * fresh, -1, keepdims=True) + 1e-06)).astype(
        jnp.bfloat16
    )
    gathered = gather_queue(queue_keys, fresh, n_q, n_dp)
    rows0 = gathered.shape[1]
    remote = gathered.reshape(-1, width)
    is_key = (jnp.arange(n_dp * rows0, dtype=jnp.int32) % rows0) < far_rows

    query = jnp.dot(query_inputs, query_weight, preferred_element_type=jnp.float32)
    inv_len = lax.rsqrt(jnp.sum(query * query, -1, keepdims=True) + 1e-06)
    unit_f = query * inv_len
    unit = unit_f.astype(jnp.bfloat16)

    dims = (((1,), (1,)), ((), ()))
    near = lax.dot_general(unit, queue_keys, dims, preferred_element_type=jnp.float32) / temper
    far = lax.dot_general(unit, remote, dims, preferred_element_type=jnp.float32) / temper
    far = jnp.where(is_key[None, :], far, -jnp.inf)
    top = jnp.maximum(jnp.max(near, -1), jnp.max(far, -1))
    e_near = jnp.exp(near - top[:, None])
    e_far = jnp.exp(far - top[:, None])
    total = jnp.sum(e_near, -1) + jnp.sum(e_far, -1)
    mixture = jnp.dot(
        e_near.astype(jnp.bfloat16), queue_keys, preferred_element_type=jnp.float32
    ) + jnp.dot(e_far.astype(jnp.bfloat16), remote, preferred_element_type=jnp.float32)

    j = positive_index
    q_src = j // k_dev
    within = j % k_dev
    local = q_src == q
    e = dp ^ (within // piece_rows)
    s = (q - q_src) % n_q
    far_at = e * rows0 + (s - 1) * piece_rows + within % piece_rows
    pick_near = (local[:, None] & (within[:, None] == jnp.arange(k_dev)[None, :])).astype(
        jnp.bfloat16
    )
    pick_far = (
        (~local)[:, None] & (far_at[:, None] == jnp.arange(n_dp * rows0)[None, :])
    ).astype(jnp.bfloat16)
    chosen = jnp.dot(pick_near, queue_keys, preferred_element_type=jnp.float32) + jnp.dot(
        pick_far, remote, preferred_element_type=jnp.float32
    )

    mixture = mixture / total[:, None]
    positive = jnp.sum(unit.astype(jnp.float32) * chosen, -1) / temper
    loss = top + jnp.log(total) - positive
    grad_unit = (mixture - chosen) / temper
    grad_query = (
        (grad_unit - unit_f * jnp.sum(unit_f * grad_unit, -1, keepdims=True)) * inv_len
    ).astype(jnp.bfloat16)
    grad_rows = reduce_scatter_grad(query_inputs, grad_query, n_q, n_dp)

    n_blocks = slot_owner.shape[0]
    slots_here = q * n_dp + jnp.arange(n_dp, dtype=jnp.int32)
    match = slot_owner[None, :] == slots_here[:, None]
    owner_block = jnp.sum(jnp.where(match, jnp.arange(n_blocks, dtype=jnp.int32)[None, :], 0), -1)
    offset = (jnp.arange(k_dev, dtype=jnp.int32) - write_pointer[0]) % k_dev
    live = offset < n_dp * new_dev
    sub_block = jnp.minimum(offset // new_dev, n_dp - 1)
    b = jnp.take(owner_block, sub_block)
    b_e = dp ^ (b % n_dp)
    b_s = (q - b // n_dp) % n_q
    source = b_e * rows0 + far_rows + b_s * new_dev + offset % new_dev
    new_queue = jnp.where(live[:, None], jnp.take(remote, source, axis=0), queue_keys)
    return (loss, grad_rows, new_queue)


def solution(mesh):
    in_specs = (
        P(("groups", "queue", "dp"), None),
        P(("groups", "queue", "dp"), None),
        P(),
        P(),
        P(("groups", "queue"), None),
        P("groups"),
        P("groups"),
        P(("groups", "queue", "dp")),
    )
    out_specs = (
        P(("groups", "queue", "dp")),
        P(("groups", "queue", "dp"), None),
        P(("groups", "queue"), None),
    )
    return jax.shard_map(body, mesh=mesh, in_specs=in_specs, out_specs=out_specs, check_vma=False)
```

```python
import jax
import jax.numpy as jnp
from jax import lax
from jax.sharding import PartitionSpec as P

temper = 0.05


def shift(x, axis, n, step):
    return lax.ppermute(x, axis, [(i, (i + step) % n) for i in range(n)])


def swap(x, axis, n, bit):
    return lax.ppermute(x, axis, [(i, i ^ bit) for i in range(n)])


def dp_bits(n_dp):
    bits = []
    b = n_dp // 2
    while b >= 1:
        bits.append(b)
        b //= 2
    return bits


def gather_queue(queue_keys, fresh, n_q, n_dp):
    dp = lax.axis_index("dp")
    k_dev, width = queue_keys.shape
    piece_rows = k_dev // n_dp
    piece = lax.dynamic_slice_in_dim(queue_keys, dp * piece_rows, piece_rows, 0)
    packed = jnp.concatenate([piece, fresh], axis=0)
    got = [shift(packed, "queue", n_q, s) for s in range(1, n_q)]
    payload = jnp.concatenate(
        [g[:piece_rows] for g in got] + [fresh] + [g[piece_rows:] for g in got], axis=0
    )
    for t, bit in enumerate(dp_bits(n_dp)):
        payload = jnp.stack([payload, swap(payload, "dp", n_dp, bit)], axis=t)
    return payload.reshape(n_dp, -1, width)


def reduce_scatter_grad(query_inputs, grad_query, n_q, n_dp):
    q = lax.axis_index("queue")
    dp = lax.axis_index("dp")
    q_dev, rows = query_inputs.shape
    width = grad_query.shape[1]
    share = rows // (n_q * n_dp)
    bits = dp_bits(n_dp)
    hb = bits[0]
    side = dp // hb
    x4 = query_inputs.reshape(q_dev, n_q, 2, hb * share)
    mine = lax.dynamic_index_in_dim(x4, side, 2, keepdims=False)
    other = lax.dynamic_index_in_dim(x4, 1 - side, 2, keepdims=False)
    got_x = swap(other, "dp", n_dp, hb)
    xs = jnp.concatenate([mine, got_x], axis=0).reshape(2 * q_dev, n_q * hb * share)
    rest = bits[1:]
    halves = 2
    cols = width // halves
    out = []
    for h in range(halves):
        g_h = grad_query[:, h * cols:(h + 1) * cols]
        gs = jnp.concatenate([g_h, swap(g_h, "dp", n_dp, hb)], axis=0)
        term = lax.dot_general(xs, gs, (((0,), (0,)), ((), ())), preferred_element_type=jnp.float32)
        t = term.reshape((n_q,) + (2,) * len(rest) + (share, cols))
        for axis in reversed(range(len(rest))):
            bit = rest[axis]
            me = (dp // bit) % 2
            keep = lax.dynamic_index_in_dim(t, me, 1 + axis, keepdims=False)
            send = lax.dynamic_index_in_dim(t, 1 - me, 1 + axis, keepdims=False)
            t = keep + swap(send, "dp", n_dp, bit)
        t = t.reshape(n_q, share, cols)
        acc = lax.dynamic_index_in_dim(t, q, 0, keepdims=False)
        for s in range(1, n_q):
            part = lax.dynamic_index_in_dim(t, (q + s) % n_q, 0, keepdims=False)
            acc = acc + shift(part, "queue", n_q, s)
        out.append(acc)
    return jnp.concatenate(out, axis=1)


def body(
    query_inputs,
    key_inputs,
    query_weight,
    key_weight,
    queue_keys,
    write_pointer,
    slot_owner,
    positive_index,
):
    q_dev, width = query_inputs.shape
    k_dev = queue_keys.shape[0]
    new_dev = key_inputs.shape[0]
    n_dp = lax.axis_size("dp")
    n_q = lax.axis_size("queue")
    q = lax.axis_index("queue")
    dp = lax.axis_index("dp")
    piece_rows = k_dev // n_dp
    far_rows = (n_q - 1) * piece_rows

    fresh = jnp.dot(key_inputs, key_weight, preferred_element_type=jnp.float32)
    fresh = (fresh * lax.rsqrt(jnp.sum(fresh * fresh, -1, keepdims=True) + 1e-06)).astype(
        jnp.bfloat16
    )
    gathered = gather_queue(queue_keys, fresh, n_q, n_dp)
    rows0 = gathered.shape[1]
    remote = gathered.reshape(-1, width)
    is_key = (jnp.arange(n_dp * rows0, dtype=jnp.int32) % rows0) < far_rows

    query = jnp.dot(query_inputs, query_weight, preferred_element_type=jnp.float32)
    inv_len = lax.rsqrt(jnp.sum(query * query, -1, keepdims=True) + 1e-06)
    unit_f = query * inv_len
    unit = unit_f.astype(jnp.bfloat16)

    dims = (((1,), (1,)), ((), ()))
    near = lax.dot_general(unit, queue_keys, dims, preferred_element_type=jnp.float32) / temper
    far = lax.dot_general(unit, remote, dims, preferred_element_type=jnp.float32) / temper
    far = jnp.where(is_key[None, :], far, -jnp.inf)
    top = jnp.maximum(jnp.max(near, -1), jnp.max(far, -1))
    e_near = jnp.exp(near - top[:, None])
    e_far = jnp.exp(far - top[:, None])
    total = jnp.sum(e_near, -1) + jnp.sum(e_far, -1)
    mixture = jnp.dot(
        e_near.astype(jnp.bfloat16), queue_keys, preferred_element_type=jnp.float32
    ) + jnp.dot(e_far.astype(jnp.bfloat16), remote, preferred_element_type=jnp.float32)

    j = positive_index
    q_src = j // k_dev
    within = j % k_dev
    local = q_src == q
    e = dp ^ (within // piece_rows)
    s = (q - q_src) % n_q
    far_at = e * rows0 + (s - 1) * piece_rows + within % piece_rows
    pick_near = (local[:, None] & (within[:, None] == jnp.arange(k_dev)[None, :])).astype(
        jnp.bfloat16
    )
    pick_far = (
        (~local)[:, None] & (far_at[:, None] == jnp.arange(n_dp * rows0)[None, :])
    ).astype(jnp.bfloat16)
    chosen = jnp.dot(pick_near, queue_keys, preferred_element_type=jnp.float32) + jnp.dot(
        pick_far, remote, preferred_element_type=jnp.float32
    )

    mixture = mixture / total[:, None]
    positive = jnp.sum(unit.astype(jnp.float32) * chosen, -1) / temper
    loss = top + jnp.log(total) - positive
    grad_unit = (mixture - chosen) / temper
    grad_query = (
        (grad_unit - unit_f * jnp.sum(unit_f * grad_unit, -1, keepdims=True)) * inv_len
    ).astype(jnp.bfloat16)
    grad_rows = reduce_scatter_grad(query_inputs, grad_query, n_q, n_dp)

    n_blocks = slot_owner.shape[0]
    slots_here = q * n_dp + jnp.arange(n_dp, dtype=jnp.int32)
    match = slot_owner[None, :] == slots_here[:, None]
    owner_block = jnp.sum(jnp.where(match, jnp.arange(n_blocks, dtype=jnp.int32)[None, :], 0), -1)
    offset = (jnp.arange(k_dev, dtype=jnp.int32) - write_pointer[0]) % k_dev
    live = offset < n_dp * new_dev
    sub_block = jnp.minimum(offset // new_dev, n_dp - 1)
    b = jnp.take(owner_block, sub_block)
    b_e = dp ^ (b % n_dp)
    b_s = (q - b // n_dp) % n_q
    source = b_e * rows0 + far_rows + b_s * new_dev + offset % new_dev
    new_queue = jnp.where(live[:, None], jnp.take(remote, source, axis=0), queue_keys)
    return (loss, grad_rows, new_queue)


def solution(mesh):
    in_specs = (
        P(("groups", "queue", "dp"), None),
        P(("groups", "queue", "dp"), None),
        P(),
        P(),
        P(("groups", "queue"), None),
        P("groups"),
        P("groups"),
        P(("groups", "queue", "dp")),
    )
    out_specs = (
        P(("groups", "queue", "dp")),
        P(("groups", "queue", "dp"), None),
        P(("groups", "queue"), None),
    )
    return jax.shard_map(body, mesh=mesh, in_specs=in_specs, out_specs=out_specs, check_vma=False)
```

```python
import jax
import jax.numpy as jnp
from jax import lax
from jax.sharding import PartitionSpec as P

temper = 0.05


def shift(x, axis, n, step):
    return lax.ppermute(x, axis, [(i, (i + step) % n) for i in range(n)])


def swap(x, axis, n, bit):
    return lax.ppermute(x, axis, [(i, i ^ bit) for i in range(n)])


def dp_bits(n_dp):
    bits = []
    b = n_dp // 2
    while b >= 1:
        bits.append(b)
        b //= 2
    return bits


def gather_queue(queue_keys, key_inputs, n_q, n_dp, halves):
    dp = lax.axis_index("dp")
    k_dev, width = queue_keys.shape
    piece_rows = k_dev // n_dp
    cols = width // halves
    piece = lax.dynamic_slice_in_dim(queue_keys, dp * piece_rows, piece_rows, 0)
    out = []
    for h in range(halves):
        mine = key_inputs[:, h * cols:(h + 1) * cols]
        packed = jnp.concatenate([piece[:, h * cols:(h + 1) * cols], mine], axis=0)
        got = [shift(packed, "queue", n_q, s) for s in range(1, n_q)]
        payload = jnp.concatenate(
            [g[:piece_rows] for g in got] + [mine] + [g[piece_rows:] for g in got], axis=0
        )
        for t, bit in enumerate(dp_bits(n_dp)):
            payload = jnp.stack([payload, swap(payload, "dp", n_dp, bit)], axis=t)
        out.append(payload.reshape(n_dp, -1, cols))
    return out


def reduce_scatter_grad(query_inputs, grad_query, n_q, n_dp):
    q = lax.axis_index("queue")
    dp = lax.axis_index("dp")
    q_dev, rows = query_inputs.shape
    width = grad_query.shape[1]
    share = rows // (n_q * n_dp)
    bits = dp_bits(n_dp)
    hb = bits[0]
    side = dp // hb
    x4 = query_inputs.reshape(q_dev, n_q, 2, hb * share)
    mine = lax.dynamic_index_in_dim(x4, side, 2, keepdims=False)
    other = lax.dynamic_index_in_dim(x4, 1 - side, 2, keepdims=False)
    got_x = swap(other, "dp", n_dp, hb)
    xs = jnp.concatenate([mine, got_x], axis=0).reshape(2 * q_dev, n_q * hb * share)
    rest = bits[1:]
    halves = 2
    cols = width // halves
    out = []
    for h in range(halves):
        g_h = grad_query[:, h * cols:(h + 1) * cols]
        gs = jnp.concatenate([g_h, swap(g_h, "dp", n_dp, hb)], axis=0)
        term = lax.dot_general(xs, gs, (((0,), (0,)), ((), ())), preferred_element_type=jnp.float32)
        t = term.reshape((n_q,) + (2,) * len(rest) + (share, cols))
        for axis in reversed(range(len(rest))):
            bit = rest[axis]
            me = (dp // bit) % 2
            keep = lax.dynamic_index_in_dim(t, me, 1 + axis, keepdims=False)
            send = lax.dynamic_index_in_dim(t, 1 - me, 1 + axis, keepdims=False)
            t = keep + swap(send, "dp", n_dp, bit)
        t = t.reshape(n_q, share, cols)
        acc = lax.dynamic_index_in_dim(t, q, 0, keepdims=False)
        for s in range(1, n_q):
            part = lax.dynamic_index_in_dim(t, (q + s) % n_q, 0, keepdims=False)
            acc = acc + shift(part, "queue", n_q, s)
        out.append(acc)
    return jnp.concatenate(out, axis=1)


def body(
    query_inputs,
    key_inputs,
    query_weight,
    key_weight,
    queue_keys,
    write_pointer,
    slot_owner,
    positive_index,
):
    q_dev, width = query_inputs.shape
    k_dev = queue_keys.shape[0]
    new_dev = key_inputs.shape[0]
    n_dp = lax.axis_size("dp")
    n_q = lax.axis_size("queue")
    q = lax.axis_index("queue")
    dp = lax.axis_index("dp")
    piece_rows = k_dev // n_dp
    far_rows = (n_q - 1) * piece_rows

    halves = 2
    cols = width // halves
    gathered = gather_queue(queue_keys, key_inputs, n_q, n_dp, halves)
    rows0 = gathered[0].shape[1]
    n_far = n_dp * rows0
    remote = [g.reshape(n_far, cols) for g in gathered]
    is_key = (jnp.arange(n_far, dtype=jnp.int32) % rows0) < far_rows

    query = jnp.dot(query_inputs, query_weight, preferred_element_type=jnp.float32)
    inv_len = lax.rsqrt(jnp.sum(query * query, -1, keepdims=True) + 1e-06)
    unit_f = query * inv_len
    unit = unit_f.astype(jnp.bfloat16)

    def by_halves(lhs, parts):
        return jnp.concatenate(
            [jnp.dot(lhs, p, preferred_element_type=jnp.float32) for p in parts], axis=1
        )

    dims = (((1,), (1,)), ((), ()))
    near = lax.dot_general(unit, queue_keys, dims, preferred_element_type=jnp.float32) / temper
    far = lax.dot_general(unit[:, :cols], remote[0], dims, preferred_element_type=jnp.float32)
    for h in range(1, halves):
        far = far + lax.dot_general(
            unit[:, h * cols:(h + 1) * cols], remote[h], dims, preferred_element_type=jnp.float32
        )
    far = jnp.where(is_key[None, :], far / temper, -jnp.inf)
    top = jnp.maximum(jnp.max(near, -1), jnp.max(far, -1))
    e_near = jnp.exp(near - top[:, None])
    e_far = jnp.exp(far - top[:, None])
    total = jnp.sum(e_near, -1) + jnp.sum(e_far, -1)
    mixture = jnp.dot(
        e_near.astype(jnp.bfloat16), queue_keys, preferred_element_type=jnp.float32
    ) + by_halves(e_far.astype(jnp.bfloat16), remote)

    j = positive_index
    q_src = j // k_dev
    within = j % k_dev
    local = q_src == q
    e = dp ^ (within // piece_rows)
    s = (q - q_src) % n_q
    far_at = e * rows0 + (s - 1) * piece_rows + within % piece_rows
    pick_near = (local[:, None] & (within[:, None] == jnp.arange(k_dev)[None, :])).astype(
        jnp.bfloat16
    )
    pick_far = ((~local)[:, None] & (far_at[:, None] == jnp.arange(n_far)[None, :])).astype(
        jnp.bfloat16
    )
    chosen = jnp.dot(pick_near, queue_keys, preferred_element_type=jnp.float32) + by_halves(
        pick_far, remote
    )

    mixture = mixture / total[:, None]
    positive = jnp.sum(unit.astype(jnp.float32) * chosen, -1) / temper
    loss = top + jnp.log(total) - positive
    grad_unit = (mixture - chosen) / temper
    grad_query = (
        (grad_unit - unit_f * jnp.sum(unit_f * grad_unit, -1, keepdims=True)) * inv_len
    ).astype(jnp.bfloat16)
    grad_rows = reduce_scatter_grad(query_inputs, grad_query, n_q, n_dp)

    n_blocks = slot_owner.shape[0]
    slots_here = q * n_dp + jnp.arange(n_dp, dtype=jnp.int32)
    match = slot_owner[None, :] == slots_here[:, None]
    owner_block = jnp.sum(jnp.where(match, jnp.arange(n_blocks, dtype=jnp.int32)[None, :], 0), -1)
    offset = (jnp.arange(k_dev, dtype=jnp.int32) - write_pointer[0]) % k_dev
    live = offset < n_dp * new_dev
    sub_block = jnp.minimum(offset // new_dev, n_dp - 1)
    b = jnp.take(owner_block, sub_block)
    b_e = dp ^ (b % n_dp)
    b_s = (q - b // n_dp) % n_q
    source = b_e * rows0 + far_rows + b_s * new_dev + offset % new_dev
    pick_new = (source[:, None] == jnp.arange(n_far)[None, :]).astype(jnp.bfloat16)
    key_rows = by_halves(pick_new, remote).astype(jnp.bfloat16)
    fresh = jnp.dot(key_rows, key_weight, preferred_element_type=jnp.float32)
    fresh = (fresh * lax.rsqrt(jnp.sum(fresh * fresh, -1, keepdims=True) + 1e-06)).astype(
        jnp.bfloat16
    )
    new_queue = jnp.where(live[:, None], fresh, queue_keys)
    return (loss, grad_rows, new_queue)


def solution(mesh):
    in_specs = (
        P(("groups", "queue", "dp"), None),
        P(("groups", "queue", "dp"), None),
        P(),
        P(),
        P(("groups", "queue"), None),
        P("groups"),
        P("groups"),
        P(("groups", "queue", "dp")),
    )
    out_specs = (
        P(("groups", "queue", "dp")),
        P(("groups", "queue", "dp"), None),
        P(("groups", "queue"), None),
    )
    return jax.shard_map(body, mesh=mesh, in_specs=in_specs, out_specs=out_specs, check_vma=False)
```

```python
import jax
import jax.numpy as jnp
from jax import lax
from jax.sharding import PartitionSpec as P

temper = 0.05


def shift(x, axis, n, step):
    return lax.ppermute(x, axis, [(i, (i + step) % n) for i in range(n)])


def swap(x, axis, n, bit):
    return lax.ppermute(x, axis, [(i, i ^ bit) for i in range(n)])


def dp_bits(n_dp):
    bits = []
    b = n_dp // 2
    while b >= 1:
        bits.append(b)
        b //= 2
    return bits


def gather_queue(queue_keys, extra, n_q, n_dp):
    dp = lax.axis_index("dp")
    k_dev, width = queue_keys.shape
    piece_rows = k_dev // n_dp
    piece = lax.dynamic_slice_in_dim(queue_keys, dp * piece_rows, piece_rows, 0)
    packed = jnp.concatenate([piece, extra], axis=0)
    got = [shift(packed, "queue", n_q, s) for s in range(1, n_q)]
    payload = jnp.concatenate(
        [g[:piece_rows] for g in got] + [extra] + [g[piece_rows:] for g in got], axis=0
    )
    for t, bit in enumerate(dp_bits(n_dp)):
        payload = jnp.stack([payload, swap(payload, "dp", n_dp, bit)], axis=t)
    return payload.reshape(n_dp, -1, width)


def reduce_scatter_grad(query_inputs, grad_query, n_q, n_dp):
    q = lax.axis_index("queue")
    dp = lax.axis_index("dp")
    q_dev, rows = query_inputs.shape
    width = grad_query.shape[1]
    share = rows // (n_q * n_dp)
    bits = dp_bits(n_dp)
    hb = bits[0]
    side = dp // hb
    x4 = query_inputs.reshape(q_dev, n_q, 2, hb * share)
    mine = lax.dynamic_index_in_dim(x4, side, 2, keepdims=False)
    other = lax.dynamic_index_in_dim(x4, 1 - side, 2, keepdims=False)
    got_x = swap(other, "dp", n_dp, hb)
    xs = jnp.concatenate([mine, got_x], axis=0).reshape(2 * q_dev, n_q * hb * share)
    rest = bits[1:]
    halves = 2
    cols = width // halves
    out = []
    for h in range(halves):
        g_h = grad_query[:, h * cols:(h + 1) * cols]
        gs = jnp.concatenate([g_h, swap(g_h, "dp", n_dp, hb)], axis=0)
        term = lax.dot_general(xs, gs, (((0,), (0,)), ((), ())), preferred_element_type=jnp.float32)
        t = term.reshape((n_q,) + (2,) * len(rest) + (share, cols))
        for axis in reversed(range(len(rest))):
            bit = rest[axis]
            me = (dp // bit) % 2
            keep = lax.dynamic_index_in_dim(t, me, 1 + axis, keepdims=False)
            send = lax.dynamic_index_in_dim(t, 1 - me, 1 + axis, keepdims=False)
            t = keep + swap(send, "dp", n_dp, bit)
        t = t.reshape(n_q, share, cols)
        bit = 1
        while bit < n_q:
            me = (q // bit) % 2
            v = t.reshape(t.shape[0] // 2, 2, share, cols)
            keep = lax.dynamic_index_in_dim(v, me, 1, keepdims=False)
            send = lax.dynamic_index_in_dim(v, 1 - me, 1, keepdims=False)
            t = keep + swap(send, "queue", n_q, bit)
            bit *= 2
        out.append(t.reshape(share, cols))
    return jnp.concatenate(out, axis=1)


def body(
    query_inputs,
    key_inputs,
    query_weight,
    key_weight,
    queue_keys,
    write_pointer,
    slot_owner,
    positive_index,
):
    q_dev, width = query_inputs.shape
    k_dev = queue_keys.shape[0]
    new_dev = key_inputs.shape[0]
    n_dp = lax.axis_size("dp")
    n_q = lax.axis_size("queue")
    q = lax.axis_index("queue")
    dp = lax.axis_index("dp")
    piece_rows = k_dev // n_dp
    far_rows = (n_q - 1) * piece_rows

    gathered = gather_queue(queue_keys, key_inputs, n_q, n_dp)
    rows0 = gathered.shape[1]
    remote = gathered.reshape(-1, width)
    is_key = (jnp.arange(n_dp * rows0, dtype=jnp.int32) % rows0) < far_rows

    query = jnp.dot(query_inputs, query_weight, preferred_element_type=jnp.float32)
    inv_len = lax.rsqrt(jnp.sum(query * query, -1, keepdims=True) + 1e-06)
    unit_f = query * inv_len
    unit = unit_f.astype(jnp.bfloat16)

    dims = (((1,), (1,)), ((), ()))
    near = lax.dot_general(unit, queue_keys, dims, preferred_element_type=jnp.float32) / temper
    far = lax.dot_general(unit, remote, dims, preferred_element_type=jnp.float32) / temper
    far = jnp.where(is_key[None, :], far, -jnp.inf)
    top = jnp.maximum(jnp.max(near, -1), jnp.max(far, -1))
    e_near = jnp.exp(near - top[:, None])
    e_far = jnp.exp(far - top[:, None])
    total = jnp.sum(e_near, -1) + jnp.sum(e_far, -1)
    mixture = jnp.dot(
        e_near.astype(jnp.bfloat16), queue_keys, preferred_element_type=jnp.float32
    ) + jnp.dot(e_far.astype(jnp.bfloat16), remote, preferred_element_type=jnp.float32)

    j = positive_index
    q_src = j // k_dev
    within = j % k_dev
    local = q_src == q
    e = dp ^ (within // piece_rows)
    s = (q - q_src) % n_q
    far_at = e * rows0 + (s - 1) * piece_rows + within % piece_rows
    pick_near = (local[:, None] & (within[:, None] == jnp.arange(k_dev)[None, :])).astype(
        jnp.bfloat16
    )
    pick_far = (
        (~local)[:, None] & (far_at[:, None] == jnp.arange(n_dp * rows0)[None, :])
    ).astype(jnp.bfloat16)
    chosen = jnp.dot(pick_near, queue_keys, preferred_element_type=jnp.float32) + jnp.dot(
        pick_far, remote, preferred_element_type=jnp.float32
    )

    mixture = mixture / total[:, None]
    positive = jnp.sum(unit.astype(jnp.float32) * chosen, -1) / temper
    loss = top + jnp.log(total) - positive
    grad_unit = (mixture - chosen) / temper
    grad_query = (
        (grad_unit - unit_f * jnp.sum(unit_f * grad_unit, -1, keepdims=True)) * inv_len
    ).astype(jnp.bfloat16)
    grad_rows = reduce_scatter_grad(query_inputs, grad_query, n_q, n_dp)

    n_blocks = slot_owner.shape[0]
    slots_here = q * n_dp + jnp.arange(n_dp, dtype=jnp.int32)
    match = slot_owner[None, :] == slots_here[:, None]
    owner_block = jnp.sum(jnp.where(match, jnp.arange(n_blocks, dtype=jnp.int32)[None, :], 0), -1)
    offset = (jnp.arange(k_dev, dtype=jnp.int32) - write_pointer[0]) % k_dev
    live = offset < n_dp * new_dev
    sub_block = jnp.minimum(offset // new_dev, n_dp - 1)
    b = jnp.take(owner_block, sub_block)
    b_e = dp ^ (b % n_dp)
    b_s = (q - b // n_dp) % n_q
    source = b_e * rows0 + far_rows + b_s * new_dev + offset % new_dev
    pick_new = (source[:, None] == jnp.arange(n_dp * rows0)[None, :]).astype(jnp.bfloat16)
    key_rows = jnp.dot(pick_new, remote, preferred_element_type=jnp.float32).astype(jnp.bfloat16)
    fresh = jnp.dot(key_rows, key_weight, preferred_element_type=jnp.float32)
    fresh = (fresh * lax.rsqrt(jnp.sum(fresh * fresh, -1, keepdims=True) + 1e-06)).astype(
        jnp.bfloat16
    )
    new_queue = jnp.where(live[:, None], fresh, queue_keys)
    return (loss, grad_rows, new_queue)


def solution(mesh):
    in_specs = (
        P(("groups", "queue", "dp"), None),
        P(("groups", "queue", "dp"), None),
        P(),
        P(),
        P(("groups", "queue"), None),
        P("groups"),
        P("groups"),
        P(("groups", "queue", "dp")),
    )
    out_specs = (
        P(("groups", "queue", "dp")),
        P(("groups", "queue", "dp"), None),
        P(("groups", "queue"), None),
    )
    return jax.shard_map(body, mesh=mesh, in_specs=in_specs, out_specs=out_specs, check_vma=False)
```

```python
import jax
import jax.numpy as jnp
from jax import lax
from jax.sharding import PartitionSpec as P

temper = 0.05


def shift(x, axis, n, step):
    return lax.ppermute(x, axis, [(i, (i + step) % n) for i in range(n)])


def swap(x, axis, n, bit):
    return lax.ppermute(x, axis, [(i, i ^ bit) for i in range(n)])


def dp_bits(n_dp):
    bits = []
    b = n_dp // 2
    while b >= 1:
        bits.append(b)
        b //= 2
    return bits


def gather_queue(queue_keys, fresh, n_q, n_dp):
    dp = lax.axis_index("dp")
    k_dev, width = queue_keys.shape
    piece_rows = k_dev // n_dp
    piece = lax.dynamic_slice_in_dim(queue_keys, dp * piece_rows, piece_rows, 0)
    packed = jnp.concatenate([piece, fresh], axis=0)
    got = [shift(packed, "queue", n_q, s) for s in range(1, n_q)]
    payload = jnp.concatenate(
        [g[:piece_rows] for g in got] + [fresh] + [g[piece_rows:] for g in got], axis=0
    )
    for t, bit in enumerate(dp_bits(n_dp)):
        payload = jnp.stack([payload, swap(payload, "dp", n_dp, bit)], axis=t)
    return payload.reshape(n_dp, -1, width)


def line_reduce(acc, q, n_q):
    for t in range(1, n_q):
        right = lax.dynamic_index_in_dim(acc, (q + n_q - t) % n_q, 0, keepdims=False)
        left = lax.dynamic_index_in_dim(acc, (q + t) % n_q, 0, keepdims=False)
        got_r = lax.ppermute(right, "queue", [(i, i + 1) for i in range(t)])
        got_l = lax.ppermute(left, "queue", [(i, i - 1) for i in range(n_q - t, n_q)])
        at_r = (q - 1 + n_q - t) % n_q
        at_l = (q + 1 + t) % n_q
        acc = lax.dynamic_update_index_in_dim(
            acc, lax.dynamic_index_in_dim(acc, at_r, 0, keepdims=False) + got_r, at_r, 0
        )
        acc = lax.dynamic_update_index_in_dim(
            acc, lax.dynamic_index_in_dim(acc, at_l, 0, keepdims=False) + got_l, at_l, 0
        )
    return lax.dynamic_index_in_dim(acc, q, 0, keepdims=False)


def reduce_scatter_grad(query_inputs, grad_query, n_q, n_dp):
    q = lax.axis_index("queue")
    dp = lax.axis_index("dp")
    q_dev, rows = query_inputs.shape
    width = grad_query.shape[1]
    share = rows // (n_q * n_dp)
    bits = dp_bits(n_dp)
    hb = bits[0]
    side = dp // hb
    x4 = query_inputs.reshape(q_dev, n_q, 2, hb * share)
    mine = lax.dynamic_index_in_dim(x4, side, 2, keepdims=False)
    other = lax.dynamic_index_in_dim(x4, 1 - side, 2, keepdims=False)
    got_x = swap(other, "dp", n_dp, hb)
    xs = jnp.concatenate([mine, got_x], axis=0).reshape(2 * q_dev, n_q * hb * share)
    rest = bits[1:]
    halves = 2
    cols = width // halves
    out = []
    for h in range(halves):
        g_h = grad_query[:, h * cols:(h + 1) * cols]
        gs = jnp.concatenate([g_h, swap(g_h, "dp", n_dp, hb)], axis=0)
        term = lax.dot_general(xs, gs, (((0,), (0,)), ((), ())), preferred_element_type=jnp.float32)
        t = term.reshape((n_q,) + (2,) * len(rest) + (share, cols))
        for axis in reversed(range(len(rest))):
            bit = rest[axis]
            me = (dp // bit) % 2
            keep = lax.dynamic_index_in_dim(t, me, 1 + axis, keepdims=False)
            send = lax.dynamic_index_in_dim(t, 1 - me, 1 + axis, keepdims=False)
            t = keep + swap(send, "dp", n_dp, bit)
        out.append(line_reduce(t.reshape(n_q, share, cols), q, n_q))
    return jnp.concatenate(out, axis=1)


def body(
    query_inputs,
    key_inputs,
    query_weight,
    key_weight,
    queue_keys,
    write_pointer,
    slot_owner,
    positive_index,
):
    q_dev, width = query_inputs.shape
    k_dev = queue_keys.shape[0]
    new_dev = key_inputs.shape[0]
    n_dp = lax.axis_size("dp")
    n_q = lax.axis_size("queue")
    q = lax.axis_index("queue")
    dp = lax.axis_index("dp")
    piece_rows = k_dev // n_dp
    far_rows = (n_q - 1) * piece_rows

    fresh = jnp.dot(key_inputs, key_weight, preferred_element_type=jnp.float32)
    fresh = (fresh * lax.rsqrt(jnp.sum(fresh * fresh, -1, keepdims=True) + 1e-06)).astype(
        jnp.bfloat16
    )
    gathered = gather_queue(queue_keys, fresh, n_q, n_dp)
    rows0 = gathered.shape[1]
    remote = gathered.reshape(-1, width)
    is_key = (jnp.arange(n_dp * rows0, dtype=jnp.int32) % rows0) < far_rows

    query = jnp.dot(query_inputs, query_weight, preferred_element_type=jnp.float32)
    inv_len = lax.rsqrt(jnp.sum(query * query, -1, keepdims=True) + 1e-06)
    unit_f = query * inv_len
    unit = unit_f.astype(jnp.bfloat16)

    dims = (((1,), (1,)), ((), ()))
    near = lax.dot_general(unit, queue_keys, dims, preferred_element_type=jnp.float32) / temper
    far = lax.dot_general(unit, remote, dims, preferred_element_type=jnp.float32) / temper
    far = jnp.where(is_key[None, :], far, -jnp.inf)
    top = jnp.maximum(jnp.max(near, -1), jnp.max(far, -1))
    e_near = jnp.exp(near - top[:, None])
    e_far = jnp.exp(far - top[:, None])
    total = jnp.sum(e_near, -1) + jnp.sum(e_far, -1)
    mixture = jnp.dot(
        e_near.astype(jnp.bfloat16), queue_keys, preferred_element_type=jnp.float32
    ) + jnp.dot(e_far.astype(jnp.bfloat16), remote, preferred_element_type=jnp.float32)

    j = positive_index
    q_src = j // k_dev
    within = j % k_dev
    local = q_src == q
    e = dp ^ (within // piece_rows)
    s = (q - q_src) % n_q
    far_at = e * rows0 + (s - 1) * piece_rows + within % piece_rows
    pick_near = (local[:, None] & (within[:, None] == jnp.arange(k_dev)[None, :])).astype(
        jnp.bfloat16
    )
    pick_far = (
        (~local)[:, None] & (far_at[:, None] == jnp.arange(n_dp * rows0)[None, :])
    ).astype(jnp.bfloat16)
    chosen = jnp.dot(pick_near, queue_keys, preferred_element_type=jnp.float32) + jnp.dot(
        pick_far, remote, preferred_element_type=jnp.float32
    )

    mixture = mixture / total[:, None]
    positive = jnp.sum(unit.astype(jnp.float32) * chosen, -1) / temper
    loss = top + jnp.log(total) - positive
    grad_unit = (mixture - chosen) / temper
    grad_query = (
        (grad_unit - unit_f * jnp.sum(unit_f * grad_unit, -1, keepdims=True)) * inv_len
    ).astype(jnp.bfloat16)
    grad_rows = reduce_scatter_grad(query_inputs, grad_query, n_q, n_dp)

    n_blocks = slot_owner.shape[0]
    slots_here = q * n_dp + jnp.arange(n_dp, dtype=jnp.int32)
    match = slot_owner[None, :] == slots_here[:, None]
    owner_block = jnp.sum(jnp.where(match, jnp.arange(n_blocks, dtype=jnp.int32)[None, :], 0), -1)
    offset = (jnp.arange(k_dev, dtype=jnp.int32) - write_pointer[0]) % k_dev
    live = offset < n_dp * new_dev
    sub_block = jnp.minimum(offset // new_dev, n_dp - 1)
    b = jnp.take(owner_block, sub_block)
    b_e = dp ^ (b % n_dp)
    b_s = (q - b // n_dp) % n_q
    source = b_e * rows0 + far_rows + b_s * new_dev + offset % new_dev
    pick_new = (source[:, None] == jnp.arange(n_dp * rows0)[None, :]).astype(jnp.bfloat16)
    placed = jnp.dot(pick_new, remote, preferred_element_type=jnp.float32).astype(jnp.bfloat16)
    new_queue = jnp.where(live[:, None], placed, queue_keys)
    return (loss, grad_rows, new_queue)


def solution(mesh):
    in_specs = (
        P(("groups", "queue", "dp"), None),
        P(("groups", "queue", "dp"), None),
        P(),
        P(),
        P(("groups", "queue"), None),
        P("groups"),
        P("groups"),
        P(("groups", "queue", "dp")),
    )
    out_specs = (
        P(("groups", "queue", "dp")),
        P(("groups", "queue", "dp"), None),
        P(("groups", "queue"), None),
    )
    return jax.shard_map(body, mesh=mesh, in_specs=in_specs, out_specs=out_specs, check_vma=False)
```

```python
import jax
import jax.numpy as jnp
from jax import lax
from jax.sharding import PartitionSpec as P

temper = 0.05


def shift(x, axis, n, step):
    return lax.ppermute(x, axis, [(i, (i + step) % n) for i in range(n)])


def swap(x, axis, n, bit):
    return lax.ppermute(x, axis, [(i, i ^ bit) for i in range(n)])


def dp_bits(n_dp):
    bits = []
    b = n_dp // 2
    while b >= 1:
        bits.append(b)
        b //= 2
    return bits


def gather_queue(queue_keys, n_q, n_dp):
    dp = lax.axis_index("dp")
    k_dev, width = queue_keys.shape
    piece_rows = k_dev // n_dp
    piece = lax.dynamic_slice_in_dim(queue_keys, dp * piece_rows, piece_rows, 0)
    payload = jnp.stack([shift(piece, "queue", n_q, s) for s in range(1, n_q)])
    for t, bit in enumerate(dp_bits(n_dp)):
        payload = jnp.stack([payload, swap(payload, "dp", n_dp, bit)], axis=t)
    return payload.reshape(-1, width)


def gather_blocks(block, n_q, n_dp):
    got = jnp.stack([block] + [shift(block, "queue", n_q, s) for s in range(1, n_q)])
    for t, bit in enumerate(dp_bits(n_dp)):
        got = jnp.stack([got, swap(got, "dp", n_dp, bit)], axis=t)
    return got.reshape(n_dp * n_q * block.shape[0], block.shape[1])


def reduce_scatter_grad(query_inputs, grad_query, n_q, n_dp):
    q = lax.axis_index("queue")
    dp = lax.axis_index("dp")
    q_dev, rows = query_inputs.shape
    width = grad_query.shape[1]
    share = rows // (n_q * n_dp)
    bits = dp_bits(n_dp)
    hb = bits[0]
    side = dp // hb
    x4 = query_inputs.reshape(q_dev, n_q, 2, hb * share)
    mine = lax.dynamic_index_in_dim(x4, side, 2, keepdims=False)
    other = lax.dynamic_index_in_dim(x4, 1 - side, 2, keepdims=False)
    got_x = swap(other, "dp", n_dp, hb)
    xs = jnp.concatenate([mine, got_x], axis=0).reshape(2 * q_dev, n_q * hb * share)
    rest = bits[1:]
    halves = 2
    cols = width // halves
    out = []
    for h in range(halves):
        g_h = grad_query[:, h * cols:(h + 1) * cols]
        gs = jnp.concatenate([g_h, swap(g_h, "dp", n_dp, hb)], axis=0)
        term = lax.dot_general(xs, gs, (((0,), (0,)), ((), ())), preferred_element_type=jnp.float32)
        t = term.reshape((n_q,) + (2,) * len(rest) + (share, cols))
        for axis in reversed(range(len(rest))):
            bit = rest[axis]
            me = (dp // bit) % 2
            keep = lax.dynamic_index_in_dim(t, me, 1 + axis, keepdims=False)
            send = lax.dynamic_index_in_dim(t, 1 - me, 1 + axis, keepdims=False)
            t = keep + swap(send, "dp", n_dp, bit)
        t = t.reshape(n_q, share, cols)
        acc = lax.dynamic_index_in_dim(t, q, 0, keepdims=False)
        for s in range(1, n_q):
            part = lax.dynamic_index_in_dim(t, (q + s) % n_q, 0, keepdims=False)
            acc = acc + shift(part, "queue", n_q, s)
        out.append(acc)
    return jnp.concatenate(out, axis=1)


def body(
    query_inputs,
    key_inputs,
    query_weight,
    key_weight,
    queue_keys,
    write_pointer,
    slot_owner,
    positive_index,
):
    q_dev, width = query_inputs.shape
    k_dev = queue_keys.shape[0]
    new_dev = key_inputs.shape[0]
    n_dp = lax.axis_size("dp")
    n_q = lax.axis_size("queue")
    q = lax.axis_index("queue")
    dp = lax.axis_index("dp")
    piece_rows = k_dev // n_dp
    far_rows = (n_q - 1) * piece_rows

    fresh = jnp.dot(key_inputs, key_weight, preferred_element_type=jnp.float32)
    fresh = (fresh * lax.rsqrt(jnp.sum(fresh * fresh, -1, keepdims=True) + 1e-06)).astype(
        jnp.bfloat16
    )
    remote = gather_queue(queue_keys, n_q, n_dp)
    rows0 = far_rows

    query = jnp.dot(query_inputs, query_weight, preferred_element_type=jnp.float32)
    inv_len = lax.rsqrt(jnp.sum(query * query, -1, keepdims=True) + 1e-06)
    unit_f = query * inv_len
    unit = unit_f.astype(jnp.bfloat16)

    dims = (((1,), (1,)), ((), ()))
    near = lax.dot_general(unit, queue_keys, dims, preferred_element_type=jnp.float32) / temper
    far = lax.dot_general(unit, remote, dims, preferred_element_type=jnp.float32) / temper
    top = jnp.maximum(jnp.max(near, -1), jnp.max(far, -1))
    e_near = jnp.exp(near - top[:, None])
    e_far = jnp.exp(far - top[:, None])
    total = jnp.sum(e_near, -1) + jnp.sum(e_far, -1)
    mixture = jnp.dot(
        e_near.astype(jnp.bfloat16), queue_keys, preferred_element_type=jnp.float32
    ) + jnp.dot(e_far.astype(jnp.bfloat16), remote, preferred_element_type=jnp.float32)

    j = positive_index
    q_src = j // k_dev
    within = j % k_dev
    local = q_src == q
    e = dp ^ (within // piece_rows)
    s = (q - q_src) % n_q
    far_at = e * rows0 + (s - 1) * piece_rows + within % piece_rows
    pick_near = (local[:, None] & (within[:, None] == jnp.arange(k_dev)[None, :])).astype(
        jnp.bfloat16
    )
    pick_far = (
        (~local)[:, None] & (far_at[:, None] == jnp.arange(n_dp * rows0)[None, :])
    ).astype(jnp.bfloat16)
    chosen = jnp.dot(pick_near, queue_keys, preferred_element_type=jnp.float32) + jnp.dot(
        pick_far, remote, preferred_element_type=jnp.float32
    )

    mixture = mixture / total[:, None]
    positive = jnp.sum(unit.astype(jnp.float32) * chosen, -1) / temper
    loss = top + jnp.log(total) - positive
    grad_unit = (mixture - chosen) / temper
    grad_query = (
        (grad_unit - unit_f * jnp.sum(unit_f * grad_unit, -1, keepdims=True)) * inv_len
    ).astype(jnp.bfloat16)
    fresh, grad_query = lax.optimization_barrier((fresh, grad_query))
    grad_rows = reduce_scatter_grad(query_inputs, grad_query, n_q, n_dp)
    blocks = gather_blocks(fresh, n_q, n_dp)

    n_blocks = slot_owner.shape[0]
    slots_here = q * n_dp + jnp.arange(n_dp, dtype=jnp.int32)
    match = slot_owner[None, :] == slots_here[:, None]
    owner_block = jnp.sum(jnp.where(match, jnp.arange(n_blocks, dtype=jnp.int32)[None, :], 0), -1)
    offset = (jnp.arange(k_dev, dtype=jnp.int32) - write_pointer[0]) % k_dev
    live = offset < n_dp * new_dev
    sub_block = jnp.minimum(offset // new_dev, n_dp - 1)
    b = jnp.take(owner_block, sub_block)
    b_e = dp ^ (b % n_dp)
    b_s = (q - b // n_dp) % n_q
    source = (b_e * n_q + b_s) * new_dev + offset % new_dev
    pick_new = (source[:, None] == jnp.arange(blocks.shape[0])[None, :]).astype(jnp.bfloat16)
    placed = jnp.dot(pick_new, blocks, preferred_element_type=jnp.float32).astype(jnp.bfloat16)
    new_queue = jnp.where(live[:, None], placed, queue_keys)
    return (loss, grad_rows, new_queue)


def solution(mesh):
    in_specs = (
        P(("groups", "queue", "dp"), None),
        P(("groups", "queue", "dp"), None),
        P(),
        P(),
        P(("groups", "queue"), None),
        P("groups"),
        P("groups"),
        P(("groups", "queue", "dp")),
    )
    out_specs = (
        P(("groups", "queue", "dp")),
        P(("groups", "queue", "dp"), None),
        P(("groups", "queue"), None),
    )
    return jax.shard_map(body, mesh=mesh, in_specs=in_specs, out_specs=out_specs, check_vma=False)
```

```python
import jax
import jax.numpy as jnp
from jax import lax
from jax.sharding import PartitionSpec as P

temper = 0.05


def shift(x, axis, n, step):
    return lax.ppermute(x, axis, [(i, (i + step) % n) for i in range(n)])


def swap(x, axis, n, bit):
    return lax.ppermute(x, axis, [(i, i ^ bit) for i in range(n)])


def dp_bits(n_dp):
    bits = []
    b = n_dp // 2
    while b >= 1:
        bits.append(b)
        b //= 2
    return bits


def gather_queue(queue_keys, n_q, n_dp):
    dp = lax.axis_index("dp")
    k_dev, width = queue_keys.shape
    piece_rows = k_dev // n_dp
    piece = lax.dynamic_slice_in_dim(queue_keys, dp * piece_rows, piece_rows, 0)
    payload = jnp.stack([shift(piece, "queue", n_q, s) for s in range(1, n_q)])
    for t, bit in enumerate(dp_bits(n_dp)):
        payload = jnp.stack([payload, swap(payload, "dp", n_dp, bit)], axis=t)
    return payload.reshape(-1, width)


def gather_blocks(block, n_q, n_dp):
    got = jnp.stack([block] + [shift(block, "queue", n_q, s) for s in range(1, n_q)])
    for t, bit in enumerate(dp_bits(n_dp)):
        got = jnp.stack([got, swap(got, "dp", n_dp, bit)], axis=t)
    return got.reshape(n_dp * n_q * block.shape[0], block.shape[1])


def reduce_scatter_grad(query_inputs, grad_query, n_q, n_dp, held):
    q = lax.axis_index("queue")
    dp = lax.axis_index("dp")
    q_dev, rows = query_inputs.shape
    width = grad_query.shape[1]
    share = rows // (n_q * n_dp)
    bits = dp_bits(n_dp)
    hb = bits[0]
    side = dp // hb
    x4 = query_inputs.reshape(q_dev, n_q, 2, hb * share)
    mine = lax.dynamic_index_in_dim(x4, side, 2, keepdims=False)
    other = lax.dynamic_index_in_dim(x4, 1 - side, 2, keepdims=False)
    got_x = swap(other, "dp", n_dp, hb)
    xs = jnp.concatenate([mine, got_x], axis=0).reshape(2 * q_dev, n_q * hb * share)
    rest = bits[1:]
    halves = 2
    cols = width // halves
    out = []
    for h in range(halves):
        g_h = grad_query[:, h * cols:(h + 1) * cols]
        gs = jnp.concatenate([g_h, swap(g_h, "dp", n_dp, hb)], axis=0)
        term = lax.dot_general(xs, gs, (((0,), (0,)), ((), ())), preferred_element_type=jnp.float32)
        t = term.reshape((n_q,) + (2,) * len(rest) + (share, cols))
        for axis in reversed(range(len(rest))):
            bit = rest[axis]
            me = (dp // bit) % 2
            keep = lax.dynamic_index_in_dim(t, me, 1 + axis, keepdims=False)
            send = lax.dynamic_index_in_dim(t, 1 - me, 1 + axis, keepdims=False)
            t = keep + swap(send, "dp", n_dp, bit)
        t = t.reshape(n_q, share, cols)
        if h == halves - 1:
            held, t = lax.optimization_barrier((held, t))
        acc = lax.dynamic_index_in_dim(t, q, 0, keepdims=False)
        for s in range(1, n_q):
            part = lax.dynamic_index_in_dim(t, (q + s) % n_q, 0, keepdims=False)
            acc = acc + shift(part, "queue", n_q, s)
        out.append(acc)
    return jnp.concatenate(out, axis=1), held


def body(
    query_inputs,
    key_inputs,
    query_weight,
    key_weight,
    queue_keys,
    write_pointer,
    slot_owner,
    positive_index,
):
    q_dev, width = query_inputs.shape
    k_dev = queue_keys.shape[0]
    new_dev = key_inputs.shape[0]
    n_dp = lax.axis_size("dp")
    n_q = lax.axis_size("queue")
    q = lax.axis_index("queue")
    dp = lax.axis_index("dp")
    piece_rows = k_dev // n_dp
    far_rows = (n_q - 1) * piece_rows

    fresh = jnp.dot(key_inputs, key_weight, preferred_element_type=jnp.float32)
    fresh = (fresh * lax.rsqrt(jnp.sum(fresh * fresh, -1, keepdims=True) + 1e-06)).astype(
        jnp.bfloat16
    )
    remote = gather_queue(queue_keys, n_q, n_dp)
    rows0 = far_rows

    query = jnp.dot(query_inputs, query_weight, preferred_element_type=jnp.float32)
    inv_len = lax.rsqrt(jnp.sum(query * query, -1, keepdims=True) + 1e-06)
    unit_f = query * inv_len
    unit = unit_f.astype(jnp.bfloat16)

    dims = (((1,), (1,)), ((), ()))
    near = lax.dot_general(unit, queue_keys, dims, preferred_element_type=jnp.float32) / temper
    far = lax.dot_general(unit, remote, dims, preferred_element_type=jnp.float32) / temper
    top = jnp.maximum(jnp.max(near, -1), jnp.max(far, -1))
    e_near = jnp.exp(near - top[:, None])
    e_far = jnp.exp(far - top[:, None])
    total = jnp.sum(e_near, -1) + jnp.sum(e_far, -1)
    mixture = jnp.dot(
        e_near.astype(jnp.bfloat16), queue_keys, preferred_element_type=jnp.float32
    ) + jnp.dot(e_far.astype(jnp.bfloat16), remote, preferred_element_type=jnp.float32)

    j = positive_index
    q_src = j // k_dev
    within = j % k_dev
    local = q_src == q
    e = dp ^ (within // piece_rows)
    s = (q - q_src) % n_q
    far_at = e * rows0 + (s - 1) * piece_rows + within % piece_rows
    pick_near = (local[:, None] & (within[:, None] == jnp.arange(k_dev)[None, :])).astype(
        jnp.bfloat16
    )
    pick_far = (
        (~local)[:, None] & (far_at[:, None] == jnp.arange(n_dp * rows0)[None, :])
    ).astype(jnp.bfloat16)
    chosen = jnp.dot(pick_near, queue_keys, preferred_element_type=jnp.float32) + jnp.dot(
        pick_far, remote, preferred_element_type=jnp.float32
    )

    mixture = mixture / total[:, None]
    positive = jnp.sum(unit.astype(jnp.float32) * chosen, -1) / temper
    loss = top + jnp.log(total) - positive
    grad_unit = (mixture - chosen) / temper
    grad_query = (
        (grad_unit - unit_f * jnp.sum(unit_f * grad_unit, -1, keepdims=True)) * inv_len
    ).astype(jnp.bfloat16)
    grad_rows, fresh = reduce_scatter_grad(query_inputs, grad_query, n_q, n_dp, fresh)
    blocks = gather_blocks(fresh, n_q, n_dp)

    n_blocks = slot_owner.shape[0]
    slots_here = q * n_dp + jnp.arange(n_dp, dtype=jnp.int32)
    match = slot_owner[None, :] == slots_here[:, None]
    owner_block = jnp.sum(jnp.where(match, jnp.arange(n_blocks, dtype=jnp.int32)[None, :], 0), -1)
    offset = (jnp.arange(k_dev, dtype=jnp.int32) - write_pointer[0]) % k_dev
    live = offset < n_dp * new_dev
    sub_block = jnp.minimum(offset // new_dev, n_dp - 1)
    b = jnp.take(owner_block, sub_block)
    b_e = dp ^ (b % n_dp)
    b_s = (q - b // n_dp) % n_q
    source = (b_e * n_q + b_s) * new_dev + offset % new_dev
    pick_new = (source[:, None] == jnp.arange(blocks.shape[0])[None, :]).astype(jnp.bfloat16)
    placed = jnp.dot(pick_new, blocks, preferred_element_type=jnp.float32).astype(jnp.bfloat16)
    new_queue = jnp.where(live[:, None], placed, queue_keys)
    return (loss, grad_rows, new_queue)


def solution(mesh):
    in_specs = (
        P(("groups", "queue", "dp"), None),
        P(("groups", "queue", "dp"), None),
        P(),
        P(),
        P(("groups", "queue"), None),
        P("groups"),
        P("groups"),
        P(("groups", "queue", "dp")),
    )
    out_specs = (
        P(("groups", "queue", "dp")),
        P(("groups", "queue", "dp"), None),
        P(("groups", "queue"), None),
    )
    return jax.shard_map(body, mesh=mesh, in_specs=in_specs, out_specs=out_specs, check_vma=False)
```

```python
import jax
import jax.numpy as jnp
from jax import lax
from jax.sharding import PartitionSpec as P

temper = 0.05


def shift(x, axis, n, step):
    return lax.ppermute(x, axis, [(i, (i + step) % n) for i in range(n)])


def swap(x, axis, n, bit):
    return lax.ppermute(x, axis, [(i, i ^ bit) for i in range(n)])


def dp_bits(n_dp):
    bits = []
    b = n_dp // 2
    while b >= 1:
        bits.append(b)
        b //= 2
    return bits


def gather_queue(queue_keys, n_q, n_dp):
    dp = lax.axis_index("dp")
    k_dev, width = queue_keys.shape
    piece_rows = k_dev // n_dp
    piece = lax.dynamic_slice_in_dim(queue_keys, dp * piece_rows, piece_rows, 0)
    payload = jnp.stack([shift(piece, "queue", n_q, s) for s in range(1, n_q)])
    for t, bit in enumerate(dp_bits(n_dp)):
        payload = jnp.stack([payload, swap(payload, "dp", n_dp, bit)], axis=t)
    return payload.reshape(-1, width)


def gather_blocks(block, n_q, n_dp):
    got = jnp.stack([block] + [shift(block, "queue", n_q, s) for s in range(1, n_q)])
    for t, bit in enumerate(dp_bits(n_dp)):
        got = jnp.stack([got, swap(got, "dp", n_dp, bit)], axis=t)
    return got.reshape(n_dp * n_q * block.shape[0], block.shape[1])


def reduce_scatter_grad(query_inputs, grad_query, n_q, n_dp):
    q = lax.axis_index("queue")
    dp = lax.axis_index("dp")
    q_dev, rows = query_inputs.shape
    width = grad_query.shape[1]
    share = rows // (n_q * n_dp)
    bits = dp_bits(n_dp)
    hb = bits[0]
    side = dp // hb
    x4 = query_inputs.reshape(q_dev, n_q, 2, hb * share)
    mine = lax.dynamic_index_in_dim(x4, side, 2, keepdims=False)
    other = lax.dynamic_index_in_dim(x4, 1 - side, 2, keepdims=False)
    got_x = swap(other, "dp", n_dp, hb)
    xs = jnp.concatenate([mine, got_x], axis=0).reshape(2 * q_dev, n_q * hb * share)
    rest = bits[1:]
    halves = 2
    cols = width // halves
    out = []
    got = None
    for h in range(halves):
        g_h = grad_query[:, h * cols:(h + 1) * cols]
        if got is not None:
            g_h, got = lax.optimization_barrier((g_h, got))
        got = swap(g_h, "dp", n_dp, hb)
        gs = jnp.concatenate([g_h, got], axis=0)
        term = lax.dot_general(xs, gs, (((0,), (0,)), ((), ())), preferred_element_type=jnp.float32)
        t = term.reshape((n_q,) + (2,) * len(rest) + (share, cols))
        for axis in reversed(range(len(rest))):
            bit = rest[axis]
            me = (dp // bit) % 2
            keep = lax.dynamic_index_in_dim(t, me, 1 + axis, keepdims=False)
            send = lax.dynamic_index_in_dim(t, 1 - me, 1 + axis, keepdims=False)
            t = keep + swap(send, "dp", n_dp, bit)
        t = t.reshape(n_q, share, cols)
        acc = lax.dynamic_index_in_dim(t, q, 0, keepdims=False)
        for s in range(1, n_q):
            part = lax.dynamic_index_in_dim(t, (q + s) % n_q, 0, keepdims=False)
            acc = acc + shift(part, "queue", n_q, s)
        out.append(acc)
    return jnp.concatenate(out, axis=1)


def body(
    query_inputs,
    key_inputs,
    query_weight,
    key_weight,
    queue_keys,
    write_pointer,
    slot_owner,
    positive_index,
):
    q_dev, width = query_inputs.shape
    k_dev = queue_keys.shape[0]
    new_dev = key_inputs.shape[0]
    n_dp = lax.axis_size("dp")
    n_q = lax.axis_size("queue")
    q = lax.axis_index("queue")
    dp = lax.axis_index("dp")
    piece_rows = k_dev // n_dp
    far_rows = (n_q - 1) * piece_rows

    fresh = jnp.dot(key_inputs, key_weight, preferred_element_type=jnp.float32)
    fresh = (fresh * lax.rsqrt(jnp.sum(fresh * fresh, -1, keepdims=True) + 1e-06)).astype(
        jnp.bfloat16
    )
    remote = gather_queue(queue_keys, n_q, n_dp)
    rows0 = far_rows

    query = jnp.dot(query_inputs, query_weight, preferred_element_type=jnp.float32)
    inv_len = lax.rsqrt(jnp.sum(query * query, -1, keepdims=True) + 1e-06)
    unit_f = query * inv_len
    unit = unit_f.astype(jnp.bfloat16)

    dims = (((1,), (1,)), ((), ()))
    near = lax.dot_general(unit, queue_keys, dims, preferred_element_type=jnp.float32) / temper
    far = lax.dot_general(unit, remote, dims, preferred_element_type=jnp.float32) / temper
    top = jnp.maximum(jnp.max(near, -1), jnp.max(far, -1))
    e_near = jnp.exp(near - top[:, None])
    e_far = jnp.exp(far - top[:, None])
    total = jnp.sum(e_near, -1) + jnp.sum(e_far, -1)
    mixture = jnp.dot(
        e_near.astype(jnp.bfloat16), queue_keys, preferred_element_type=jnp.float32
    ) + jnp.dot(e_far.astype(jnp.bfloat16), remote, preferred_element_type=jnp.float32)

    j = positive_index
    q_src = j // k_dev
    within = j % k_dev
    local = q_src == q
    e = dp ^ (within // piece_rows)
    s = (q - q_src) % n_q
    far_at = e * rows0 + (s - 1) * piece_rows + within % piece_rows
    pick_near = (local[:, None] & (within[:, None] == jnp.arange(k_dev)[None, :])).astype(
        jnp.bfloat16
    )
    pick_far = (
        (~local)[:, None] & (far_at[:, None] == jnp.arange(n_dp * rows0)[None, :])
    ).astype(jnp.bfloat16)
    chosen = jnp.dot(pick_near, queue_keys, preferred_element_type=jnp.float32) + jnp.dot(
        pick_far, remote, preferred_element_type=jnp.float32
    )

    mixture = mixture / total[:, None]
    positive = jnp.sum(unit.astype(jnp.float32) * chosen, -1) / temper
    loss = top + jnp.log(total) - positive
    grad_unit = (mixture - chosen) / temper
    grad_query = (
        (grad_unit - unit_f * jnp.sum(unit_f * grad_unit, -1, keepdims=True)) * inv_len
    ).astype(jnp.bfloat16)
    fresh, grad_query = lax.optimization_barrier((fresh, grad_query))
    grad_rows = reduce_scatter_grad(query_inputs, grad_query, n_q, n_dp)
    blocks = gather_blocks(fresh, n_q, n_dp)

    n_blocks = slot_owner.shape[0]
    slots_here = q * n_dp + jnp.arange(n_dp, dtype=jnp.int32)
    match = slot_owner[None, :] == slots_here[:, None]
    owner_block = jnp.sum(jnp.where(match, jnp.arange(n_blocks, dtype=jnp.int32)[None, :], 0), -1)
    offset = (jnp.arange(k_dev, dtype=jnp.int32) - write_pointer[0]) % k_dev
    live = offset < n_dp * new_dev
    sub_block = jnp.minimum(offset // new_dev, n_dp - 1)
    b = jnp.take(owner_block, sub_block)
    b_e = dp ^ (b % n_dp)
    b_s = (q - b // n_dp) % n_q
    source = (b_e * n_q + b_s) * new_dev + offset % new_dev
    pick_new = (source[:, None] == jnp.arange(blocks.shape[0])[None, :]).astype(jnp.bfloat16)
    placed = jnp.dot(pick_new, blocks, preferred_element_type=jnp.float32).astype(jnp.bfloat16)
    new_queue = jnp.where(live[:, None], placed, queue_keys)
    return (loss, grad_rows, new_queue)


def solution(mesh):
    in_specs = (
        P(("groups", "queue", "dp"), None),
        P(("groups", "queue", "dp"), None),
        P(),
        P(),
        P(("groups", "queue"), None),
        P("groups"),
        P("groups"),
        P(("groups", "queue", "dp")),
    )
    out_specs = (
        P(("groups", "queue", "dp")),
        P(("groups", "queue", "dp"), None),
        P(("groups", "queue"), None),
    )
    return jax.shard_map(body, mesh=mesh, in_specs=in_specs, out_specs=out_specs, check_vma=False)
```

```python
import jax
import jax.numpy as jnp
from jax import lax
from jax.sharding import PartitionSpec as P

temper = 0.05


def shift(x, axis, n, step):
    return lax.ppermute(x, axis, [(i, (i + step) % n) for i in range(n)])


def swap(x, axis, n, bit):
    return lax.ppermute(x, axis, [(i, i ^ bit) for i in range(n)])


def dp_bits(n_dp):
    bits = []
    b = n_dp // 2
    while b >= 1:
        bits.append(b)
        b //= 2
    return bits


def gather_queue(queue_keys, n_q, n_dp):
    dp = lax.axis_index("dp")
    k_dev, width = queue_keys.shape
    piece_rows = k_dev // n_dp
    piece = lax.dynamic_slice_in_dim(queue_keys, dp * piece_rows, piece_rows, 0)
    payload = jnp.stack([shift(piece, "queue", n_q, s) for s in range(1, n_q)])
    for t, bit in enumerate(dp_bits(n_dp)):
        payload = jnp.stack([payload, swap(payload, "dp", n_dp, bit)], axis=t)
    return payload.reshape(-1, width)


def gather_blocks(block, n_q, n_dp):
    got = jnp.stack([block] + [shift(block, "queue", n_q, s) for s in range(1, n_q)])
    for t, bit in enumerate(dp_bits(n_dp)):
        got = jnp.stack([got, swap(got, "dp", n_dp, bit)], axis=t)
    return got.reshape(n_dp * n_q * block.shape[0], block.shape[1])


def reduce_scatter_grad(query_inputs, grad_query, n_q, n_dp):
    q = lax.axis_index("queue")
    dp = lax.axis_index("dp")
    q_dev, rows = query_inputs.shape
    width = grad_query.shape[1]
    share = rows // (n_q * n_dp)
    bits = dp_bits(n_dp)
    hb = bits[0]
    side = dp // hb
    x4 = query_inputs.reshape(q_dev, n_q, 2, hb * share)
    mine = lax.dynamic_index_in_dim(x4, side, 2, keepdims=False)
    other = lax.dynamic_index_in_dim(x4, 1 - side, 2, keepdims=False)
    got_x = swap(other, "dp", n_dp, hb)
    xs = jnp.concatenate([mine, got_x], axis=0).reshape(2 * q_dev, n_q * hb * share)
    rest = bits[1:]
    halves = 2
    cols = width // halves
    out = []
    for h in range(halves):
        g_h = grad_query[:, h * cols:(h + 1) * cols]
        gs = jnp.concatenate([g_h, swap(g_h, "dp", n_dp, hb)], axis=0)
        term = lax.dot_general(xs, gs, (((0,), (0,)), ((), ())), preferred_element_type=jnp.float32)
        t = term.reshape((n_q,) + (2,) * len(rest) + (share, cols))
        for axis in reversed(range(len(rest))):
            bit = rest[axis]
            me = (dp // bit) % 2
            keep = lax.dynamic_index_in_dim(t, me, 1 + axis, keepdims=False)
            send = lax.dynamic_index_in_dim(t, 1 - me, 1 + axis, keepdims=False)
            t = keep + swap(send, "dp", n_dp, bit)
        t = t.reshape(n_q, share, cols)
        acc = lax.dynamic_index_in_dim(t, q, 0, keepdims=False)
        for s in range(1, n_q):
            part = lax.dynamic_index_in_dim(t, (q + s) % n_q, 0, keepdims=False)
            acc = acc + shift(part, "queue", n_q, s)
        out.append(acc)
    return jnp.concatenate(out, axis=1)


def body(
    query_inputs,
    key_inputs,
    query_weight,
    key_weight,
    queue_keys,
    write_pointer,
    slot_owner,
    positive_index,
):
    q_dev, width = query_inputs.shape
    k_dev = queue_keys.shape[0]
    new_dev = key_inputs.shape[0]
    n_dp = lax.axis_size("dp")
    n_q = lax.axis_size("queue")
    q = lax.axis_index("queue")
    dp = lax.axis_index("dp")
    piece_rows = k_dev // n_dp
    far_rows = (n_q - 1) * piece_rows

    blocks = gather_blocks(key_inputs, n_q, n_dp)
    remote = gather_queue(queue_keys, n_q, n_dp)
    rows0 = far_rows

    query = jnp.dot(query_inputs, query_weight, preferred_element_type=jnp.float32)
    inv_len = lax.rsqrt(jnp.sum(query * query, -1, keepdims=True) + 1e-06)
    unit_f = query * inv_len
    unit = unit_f.astype(jnp.bfloat16)

    dims = (((1,), (1,)), ((), ()))
    near = lax.dot_general(unit, queue_keys, dims, preferred_element_type=jnp.float32) / temper
    far = lax.dot_general(unit, remote, dims, preferred_element_type=jnp.float32) / temper
    top = jnp.maximum(jnp.max(near, -1), jnp.max(far, -1))
    e_near = jnp.exp(near - top[:, None])
    e_far = jnp.exp(far - top[:, None])
    total = jnp.sum(e_near, -1) + jnp.sum(e_far, -1)
    mixture = jnp.dot(
        e_near.astype(jnp.bfloat16), queue_keys, preferred_element_type=jnp.float32
    ) + jnp.dot(e_far.astype(jnp.bfloat16), remote, preferred_element_type=jnp.float32)

    j = positive_index
    q_src = j // k_dev
    within = j % k_dev
    local = q_src == q
    e = dp ^ (within // piece_rows)
    s = (q - q_src) % n_q
    far_at = e * rows0 + (s - 1) * piece_rows + within % piece_rows
    pick_near = (local[:, None] & (within[:, None] == jnp.arange(k_dev)[None, :])).astype(
        jnp.bfloat16
    )
    pick_far = (
        (~local)[:, None] & (far_at[:, None] == jnp.arange(n_dp * rows0)[None, :])
    ).astype(jnp.bfloat16)
    chosen = jnp.dot(pick_near, queue_keys, preferred_element_type=jnp.float32) + jnp.dot(
        pick_far, remote, preferred_element_type=jnp.float32
    )

    mixture = mixture / total[:, None]
    positive = jnp.sum(unit.astype(jnp.float32) * chosen, -1) / temper
    loss = top + jnp.log(total) - positive
    grad_unit = (mixture - chosen) / temper
    grad_query = (
        (grad_unit - unit_f * jnp.sum(unit_f * grad_unit, -1, keepdims=True)) * inv_len
    ).astype(jnp.bfloat16)
    grad_rows = reduce_scatter_grad(query_inputs, grad_query, n_q, n_dp)

    n_blocks = slot_owner.shape[0]
    slots_here = q * n_dp + jnp.arange(n_dp, dtype=jnp.int32)
    match = slot_owner[None, :] == slots_here[:, None]
    owner_block = jnp.sum(jnp.where(match, jnp.arange(n_blocks, dtype=jnp.int32)[None, :], 0), -1)
    offset = (jnp.arange(k_dev, dtype=jnp.int32) - write_pointer[0]) % k_dev
    live = offset < n_dp * new_dev
    sub_block = jnp.minimum(offset // new_dev, n_dp - 1)
    b = jnp.take(owner_block, sub_block)
    b_e = dp ^ (b % n_dp)
    b_s = (q - b // n_dp) % n_q
    source = (b_e * n_q + b_s) * new_dev + offset % new_dev
    pick_new = (source[:, None] == jnp.arange(blocks.shape[0])[None, :]).astype(jnp.bfloat16)
    key_rows = jnp.dot(pick_new, blocks, preferred_element_type=jnp.float32).astype(jnp.bfloat16)
    fresh = jnp.dot(key_rows, key_weight, preferred_element_type=jnp.float32)
    fresh = (fresh * lax.rsqrt(jnp.sum(fresh * fresh, -1, keepdims=True) + 1e-06)).astype(
        jnp.bfloat16
    )
    new_queue = jnp.where(live[:, None], fresh, queue_keys)
    return (loss, grad_rows, new_queue)


def solution(mesh):
    in_specs = (
        P(("groups", "queue", "dp"), None),
        P(("groups", "queue", "dp"), None),
        P(),
        P(),
        P(("groups", "queue"), None),
        P("groups"),
        P("groups"),
        P(("groups", "queue", "dp")),
    )
    out_specs = (
        P(("groups", "queue", "dp")),
        P(("groups", "queue", "dp"), None),
        P(("groups", "queue"), None),
    )
    return jax.shard_map(body, mesh=mesh, in_specs=in_specs, out_specs=out_specs, check_vma=False)
```

```python
import jax
import jax.numpy as jnp
from jax import lax
from jax.sharding import PartitionSpec as P

temper = 0.05


def shift(x, axis, n, step):
    return lax.ppermute(x, axis, [(i, (i + step) % n) for i in range(n)])


def swap(x, axis, n, bit):
    return lax.ppermute(x, axis, [(i, i ^ bit) for i in range(n)])


def dp_bits(n_dp):
    bits = []
    b = n_dp // 2
    while b >= 1:
        bits.append(b)
        b //= 2
    return bits


def gather_queue(queue_keys, n_q, n_dp):
    dp = lax.axis_index("dp")
    k_dev, width = queue_keys.shape
    piece_rows = k_dev // n_dp
    piece = lax.dynamic_slice_in_dim(queue_keys, dp * piece_rows, piece_rows, 0)
    payload = jnp.stack([shift(piece, "queue", n_q, s) for s in range(1, n_q)])
    for t, bit in enumerate(dp_bits(n_dp)):
        payload = jnp.stack([payload, swap(payload, "dp", n_dp, bit)], axis=t)
    return payload.reshape(-1, width)


def gather_blocks(block, n_q, n_dp):
    got = jnp.stack([block] + [shift(block, "queue", n_q, s) for s in range(1, n_q)])
    for t, bit in enumerate(dp_bits(n_dp)):
        got = jnp.stack([got, swap(got, "dp", n_dp, bit)], axis=t)
    return got.reshape(n_dp * n_q * block.shape[0], block.shape[1])


def reduce_scatter_grad(query_inputs, grad_query, n_q, n_dp):
    q = lax.axis_index("queue")
    dp = lax.axis_index("dp")
    q_dev, rows = query_inputs.shape
    width = grad_query.shape[1]
    share = rows // (n_q * n_dp)
    bits = dp_bits(n_dp)
    hb = bits[0]
    side = dp // hb
    x4 = query_inputs.reshape(q_dev, n_q, 2, hb * share)
    mine = lax.dynamic_index_in_dim(x4, side, 2, keepdims=False)
    other = lax.dynamic_index_in_dim(x4, 1 - side, 2, keepdims=False)
    got_x = swap(other, "dp", n_dp, hb)
    xs = jnp.concatenate([mine, got_x], axis=0).reshape(2 * q_dev, n_q * hb * share)
    rest = bits[1:]
    halves = 2
    cols = width // halves
    out = []
    for h in range(halves):
        g_h = grad_query[:, h * cols:(h + 1) * cols]
        gs = jnp.concatenate([g_h, swap(g_h, "dp", n_dp, hb)], axis=0)
        term = lax.dot_general(xs, gs, (((0,), (0,)), ((), ())), preferred_element_type=jnp.float32)
        t = term.reshape((n_q,) + (2,) * len(rest) + (share, cols))
        for axis in reversed(range(len(rest))):
            bit = rest[axis]
            me = (dp // bit) % 2
            keep = lax.dynamic_index_in_dim(t, me, 1 + axis, keepdims=False)
            send = lax.dynamic_index_in_dim(t, 1 - me, 1 + axis, keepdims=False)
            t = keep + swap(send, "dp", n_dp, bit)
        t = t.reshape(n_q, share, cols)
        out.append(jnp.sum(lax.all_to_all(t, "queue", 0, 0, tiled=False), 0))
    return jnp.concatenate(out, axis=1)


def body(
    query_inputs,
    key_inputs,
    query_weight,
    key_weight,
    queue_keys,
    write_pointer,
    slot_owner,
    positive_index,
):
    q_dev, width = query_inputs.shape
    k_dev = queue_keys.shape[0]
    new_dev = key_inputs.shape[0]
    n_dp = lax.axis_size("dp")
    n_q = lax.axis_size("queue")
    q = lax.axis_index("queue")
    dp = lax.axis_index("dp")
    piece_rows = k_dev // n_dp
    far_rows = (n_q - 1) * piece_rows

    fresh = jnp.dot(key_inputs, key_weight, preferred_element_type=jnp.float32)
    fresh = (fresh * lax.rsqrt(jnp.sum(fresh * fresh, -1, keepdims=True) + 1e-06)).astype(
        jnp.bfloat16
    )
    remote = gather_queue(queue_keys, n_q, n_dp)
    rows0 = far_rows

    query = jnp.dot(query_inputs, query_weight, preferred_element_type=jnp.float32)
    inv_len = lax.rsqrt(jnp.sum(query * query, -1, keepdims=True) + 1e-06)
    unit_f = query * inv_len
    unit = unit_f.astype(jnp.bfloat16)

    dims = (((1,), (1,)), ((), ()))
    near = lax.dot_general(unit, queue_keys, dims, preferred_element_type=jnp.float32) / temper
    far = lax.dot_general(unit, remote, dims, preferred_element_type=jnp.float32) / temper
    top = jnp.maximum(jnp.max(near, -1), jnp.max(far, -1))
    e_near = jnp.exp(near - top[:, None])
    e_far = jnp.exp(far - top[:, None])
    total = jnp.sum(e_near, -1) + jnp.sum(e_far, -1)
    mixture = jnp.dot(
        e_near.astype(jnp.bfloat16), queue_keys, preferred_element_type=jnp.float32
    ) + jnp.dot(e_far.astype(jnp.bfloat16), remote, preferred_element_type=jnp.float32)

    j = positive_index
    q_src = j // k_dev
    within = j % k_dev
    local = q_src == q
    e = dp ^ (within // piece_rows)
    s = (q - q_src) % n_q
    far_at = e * rows0 + (s - 1) * piece_rows + within % piece_rows
    pick_near = (local[:, None] & (within[:, None] == jnp.arange(k_dev)[None, :])).astype(
        jnp.bfloat16
    )
    pick_far = (
        (~local)[:, None] & (far_at[:, None] == jnp.arange(n_dp * rows0)[None, :])
    ).astype(jnp.bfloat16)
    chosen = jnp.dot(pick_near, queue_keys, preferred_element_type=jnp.float32) + jnp.dot(
        pick_far, remote, preferred_element_type=jnp.float32
    )

    mixture = mixture / total[:, None]
    positive = jnp.sum(unit.astype(jnp.float32) * chosen, -1) / temper
    loss = top + jnp.log(total) - positive
    grad_unit = (mixture - chosen) / temper
    grad_query = (
        (grad_unit - unit_f * jnp.sum(unit_f * grad_unit, -1, keepdims=True)) * inv_len
    ).astype(jnp.bfloat16)
    fresh, grad_query = lax.optimization_barrier((fresh, grad_query))
    grad_rows = reduce_scatter_grad(query_inputs, grad_query, n_q, n_dp)
    blocks = gather_blocks(fresh, n_q, n_dp)

    n_blocks = slot_owner.shape[0]
    slots_here = q * n_dp + jnp.arange(n_dp, dtype=jnp.int32)
    match = slot_owner[None, :] == slots_here[:, None]
    owner_block = jnp.sum(jnp.where(match, jnp.arange(n_blocks, dtype=jnp.int32)[None, :], 0), -1)
    offset = (jnp.arange(k_dev, dtype=jnp.int32) - write_pointer[0]) % k_dev
    live = offset < n_dp * new_dev
    sub_block = jnp.minimum(offset // new_dev, n_dp - 1)
    b = jnp.take(owner_block, sub_block)
    b_e = dp ^ (b % n_dp)
    b_s = (q - b // n_dp) % n_q
    source = (b_e * n_q + b_s) * new_dev + offset % new_dev
    pick_new = (source[:, None] == jnp.arange(blocks.shape[0])[None, :]).astype(jnp.bfloat16)
    placed = jnp.dot(pick_new, blocks, preferred_element_type=jnp.float32).astype(jnp.bfloat16)
    new_queue = jnp.where(live[:, None], placed, queue_keys)
    return (loss, grad_rows, new_queue)


def solution(mesh):
    in_specs = (
        P(("groups", "queue", "dp"), None),
        P(("groups", "queue", "dp"), None),
        P(),
        P(),
        P(("groups", "queue"), None),
        P("groups"),
        P("groups"),
        P(("groups", "queue", "dp")),
    )
    out_specs = (
        P(("groups", "queue", "dp")),
        P(("groups", "queue", "dp"), None),
        P(("groups", "queue"), None),
    )
    return jax.shard_map(body, mesh=mesh, in_specs=in_specs, out_specs=out_specs, check_vma=False)
```

```python
import jax
import jax.numpy as jnp
from jax import lax
from jax.sharding import PartitionSpec as P

temper = 0.05


def shift(x, axis, n, step):
    return lax.ppermute(x, axis, [(i, (i + step) % n) for i in range(n)])


def swap(x, axis, n, bit):
    return lax.ppermute(x, axis, [(i, i ^ bit) for i in range(n)])


def dp_bits(n_dp):
    bits = []
    b = n_dp // 2
    while b >= 1:
        bits.append(b)
        b //= 2
    return bits


def gather_queue(queue_keys, n_q, n_dp):
    dp = lax.axis_index("dp")
    k_dev, width = queue_keys.shape
    piece_rows = k_dev // n_dp
    piece = lax.dynamic_slice_in_dim(queue_keys, dp * piece_rows, piece_rows, 0)
    payload = jnp.stack([shift(piece, "queue", n_q, s) for s in range(1, n_q)])
    for t, bit in enumerate(dp_bits(n_dp)):
        payload = jnp.stack([payload, swap(payload, "dp", n_dp, bit)], axis=t)
    return payload.reshape(-1, width)


def gather_blocks(block, n_q, n_dp):
    got = jnp.stack([block] + [shift(block, "queue", n_q, s) for s in range(1, n_q)])
    for t, bit in enumerate(dp_bits(n_dp)):
        got = jnp.stack([got, swap(got, "dp", n_dp, bit)], axis=t)
    return got.reshape(n_dp * n_q * block.shape[0], block.shape[1])


def reduce_scatter_grad(query_inputs, grad_query, n_q, n_dp):
    q = lax.axis_index("queue")
    dp = lax.axis_index("dp")
    q_dev, rows = query_inputs.shape
    width = grad_query.shape[1]
    share = rows // (n_q * n_dp)
    bits = dp_bits(n_dp)
    hb = bits[0]
    side = dp // hb
    x4 = query_inputs.reshape(q_dev, n_q, 2, hb * share)
    mine = lax.dynamic_index_in_dim(x4, side, 2, keepdims=False)
    other = lax.dynamic_index_in_dim(x4, 1 - side, 2, keepdims=False)
    got_x = swap(other, "dp", n_dp, hb)
    xs = jnp.concatenate([mine, got_x], axis=0).reshape(2 * q_dev, n_q * hb * share)
    rest = bits[1:]
    halves = 4
    cols = width // halves
    out = []
    for h in range(halves):
        g_h = grad_query[:, h * cols:(h + 1) * cols]
        gs = jnp.concatenate([g_h, swap(g_h, "dp", n_dp, hb)], axis=0)
        term = lax.dot_general(xs, gs, (((0,), (0,)), ((), ())), preferred_element_type=jnp.float32)
        t = term.reshape((n_q,) + (2,) * len(rest) + (share, cols))
        for axis in reversed(range(len(rest))):
            bit = rest[axis]
            me = (dp // bit) % 2
            keep = lax.dynamic_index_in_dim(t, me, 1 + axis, keepdims=False)
            send = lax.dynamic_index_in_dim(t, 1 - me, 1 + axis, keepdims=False)
            t = keep + swap(send, "dp", n_dp, bit)
        t = t.reshape(n_q, share, cols)
        acc = lax.dynamic_index_in_dim(t, q, 0, keepdims=False)
        for s in range(1, n_q):
            part = lax.dynamic_index_in_dim(t, (q + s) % n_q, 0, keepdims=False)
            acc = acc + shift(part, "queue", n_q, s)
        out.append(acc)
    return jnp.concatenate(out, axis=1)


def body(
    query_inputs,
    key_inputs,
    query_weight,
    key_weight,
    queue_keys,
    write_pointer,
    slot_owner,
    positive_index,
):
    q_dev, width = query_inputs.shape
    k_dev = queue_keys.shape[0]
    new_dev = key_inputs.shape[0]
    n_dp = lax.axis_size("dp")
    n_q = lax.axis_size("queue")
    q = lax.axis_index("queue")
    dp = lax.axis_index("dp")
    piece_rows = k_dev // n_dp
    far_rows = (n_q - 1) * piece_rows

    fresh = jnp.dot(key_inputs, key_weight, preferred_element_type=jnp.float32)
    fresh = (fresh * lax.rsqrt(jnp.sum(fresh * fresh, -1, keepdims=True) + 1e-06)).astype(
        jnp.bfloat16
    )
    remote = gather_queue(queue_keys, n_q, n_dp)
    rows0 = far_rows

    query = jnp.dot(query_inputs, query_weight, preferred_element_type=jnp.float32)
    inv_len = lax.rsqrt(jnp.sum(query * query, -1, keepdims=True) + 1e-06)
    unit_f = query * inv_len
    unit = unit_f.astype(jnp.bfloat16)

    dims = (((1,), (1,)), ((), ()))
    near = lax.dot_general(unit, queue_keys, dims, preferred_element_type=jnp.float32) / temper
    far = lax.dot_general(unit, remote, dims, preferred_element_type=jnp.float32) / temper
    top = jnp.maximum(jnp.max(near, -1), jnp.max(far, -1))
    e_near = jnp.exp(near - top[:, None])
    e_far = jnp.exp(far - top[:, None])
    total = jnp.sum(e_near, -1) + jnp.sum(e_far, -1)
    mixture = jnp.dot(
        e_near.astype(jnp.bfloat16), queue_keys, preferred_element_type=jnp.float32
    ) + jnp.dot(e_far.astype(jnp.bfloat16), remote, preferred_element_type=jnp.float32)

    j = positive_index
    q_src = j // k_dev
    within = j % k_dev
    local = q_src == q
    e = dp ^ (within // piece_rows)
    s = (q - q_src) % n_q
    far_at = e * rows0 + (s - 1) * piece_rows + within % piece_rows
    pick_near = (local[:, None] & (within[:, None] == jnp.arange(k_dev)[None, :])).astype(
        jnp.bfloat16
    )
    pick_far = (
        (~local)[:, None] & (far_at[:, None] == jnp.arange(n_dp * rows0)[None, :])
    ).astype(jnp.bfloat16)
    chosen = jnp.dot(pick_near, queue_keys, preferred_element_type=jnp.float32) + jnp.dot(
        pick_far, remote, preferred_element_type=jnp.float32
    )

    mixture = mixture / total[:, None]
    positive = jnp.sum(unit.astype(jnp.float32) * chosen, -1) / temper
    loss = top + jnp.log(total) - positive
    grad_unit = (mixture - chosen) / temper
    grad_query = (
        (grad_unit - unit_f * jnp.sum(unit_f * grad_unit, -1, keepdims=True)) * inv_len
    ).astype(jnp.bfloat16)
    fresh, grad_query = lax.optimization_barrier((fresh, grad_query))
    grad_rows = reduce_scatter_grad(query_inputs, grad_query, n_q, n_dp)
    blocks = gather_blocks(fresh, n_q, n_dp)

    n_blocks = slot_owner.shape[0]
    slots_here = q * n_dp + jnp.arange(n_dp, dtype=jnp.int32)
    match = slot_owner[None, :] == slots_here[:, None]
    owner_block = jnp.sum(jnp.where(match, jnp.arange(n_blocks, dtype=jnp.int32)[None, :], 0), -1)
    offset = (jnp.arange(k_dev, dtype=jnp.int32) - write_pointer[0]) % k_dev
    live = offset < n_dp * new_dev
    sub_block = jnp.minimum(offset // new_dev, n_dp - 1)
    b = jnp.take(owner_block, sub_block)
    b_e = dp ^ (b % n_dp)
    b_s = (q - b // n_dp) % n_q
    source = (b_e * n_q + b_s) * new_dev + offset % new_dev
    pick_new = (source[:, None] == jnp.arange(blocks.shape[0])[None, :]).astype(jnp.bfloat16)
    placed = jnp.dot(pick_new, blocks, preferred_element_type=jnp.float32).astype(jnp.bfloat16)
    new_queue = jnp.where(live[:, None], placed, queue_keys)
    return (loss, grad_rows, new_queue)


def solution(mesh):
    in_specs = (
        P(("groups", "queue", "dp"), None),
        P(("groups", "queue", "dp"), None),
        P(),
        P(),
        P(("groups", "queue"), None),
        P("groups"),
        P("groups"),
        P(("groups", "queue", "dp")),
    )
    out_specs = (
        P(("groups", "queue", "dp")),
        P(("groups", "queue", "dp"), None),
        P(("groups", "queue"), None),
    )
    return jax.shard_map(body, mesh=mesh, in_specs=in_specs, out_specs=out_specs, check_vma=False)
```

```python
import jax
import jax.numpy as jnp
from jax import lax
from jax.sharding import PartitionSpec as P

temper = 0.05


def shift(x, axis, n, step):
    return lax.ppermute(x, axis, [(i, (i + step) % n) for i in range(n)])


def swap(x, axis, n, bit):
    return lax.ppermute(x, axis, [(i, i ^ bit) for i in range(n)])


def dp_bits(n_dp):
    bits = []
    b = n_dp // 2
    while b >= 1:
        bits.append(b)
        b //= 2
    return bits


def gather_queue(queue_keys, n_q, n_dp):
    dp = lax.axis_index("dp")
    k_dev, width = queue_keys.shape
    piece_rows = k_dev // n_dp
    piece = lax.dynamic_slice_in_dim(queue_keys, dp * piece_rows, piece_rows, 0)
    payload = jnp.stack([shift(piece, "queue", n_q, s) for s in range(1, n_q)])
    for t, bit in enumerate(dp_bits(n_dp)):
        payload = jnp.stack([payload, swap(payload, "dp", n_dp, bit)], axis=t)
    return payload.reshape(-1, width)


def blocks_over_queue(block, n_q):
    return jnp.stack([block] + [shift(block, "queue", n_q, s) for s in range(1, n_q)])


def gather_blocks(got, n_q, n_dp):
    block = got[0]
    for t, bit in enumerate(dp_bits(n_dp)):
        got = jnp.stack([got, swap(got, "dp", n_dp, bit)], axis=t)
    return got.reshape(n_dp * n_q * block.shape[0], block.shape[1])


def reduce_scatter_grad(query_inputs, grad_query, n_q, n_dp, held):
    q = lax.axis_index("queue")
    dp = lax.axis_index("dp")
    q_dev, rows = query_inputs.shape
    width = grad_query.shape[1]
    share = rows // (n_q * n_dp)
    bits = dp_bits(n_dp)
    hb = bits[0]
    side = dp // hb
    x4 = query_inputs.reshape(q_dev, n_q, 2, hb * share)
    mine = lax.dynamic_index_in_dim(x4, side, 2, keepdims=False)
    other = lax.dynamic_index_in_dim(x4, 1 - side, 2, keepdims=False)
    got_x = swap(other, "dp", n_dp, hb)
    xs = jnp.concatenate([mine, got_x], axis=0).reshape(2 * q_dev, n_q * hb * share)
    rest = bits[1:]
    halves = 2
    cols = width // halves
    out = []
    for h in range(halves):
        g_h = grad_query[:, h * cols:(h + 1) * cols]
        got_g = swap(g_h, "dp", n_dp, hb)
        if h == halves - 1:
            held, got_g = lax.optimization_barrier((held, got_g))
        gs = jnp.concatenate([g_h, got_g], axis=0)
        term = lax.dot_general(xs, gs, (((0,), (0,)), ((), ())), preferred_element_type=jnp.float32)
        t = term.reshape((n_q,) + (2,) * len(rest) + (share, cols))
        for axis in reversed(range(len(rest))):
            bit = rest[axis]
            me = (dp // bit) % 2
            keep = lax.dynamic_index_in_dim(t, me, 1 + axis, keepdims=False)
            send = lax.dynamic_index_in_dim(t, 1 - me, 1 + axis, keepdims=False)
            t = keep + swap(send, "dp", n_dp, bit)
        t = t.reshape(n_q, share, cols)
        acc = lax.dynamic_index_in_dim(t, q, 0, keepdims=False)
        for s in range(1, n_q):
            part = lax.dynamic_index_in_dim(t, (q + s) % n_q, 0, keepdims=False)
            acc = acc + shift(part, "queue", n_q, s)
        out.append(acc)
    return jnp.concatenate(out, axis=1), held


def body(
    query_inputs,
    key_inputs,
    query_weight,
    key_weight,
    queue_keys,
    write_pointer,
    slot_owner,
    positive_index,
):
    q_dev, width = query_inputs.shape
    k_dev = queue_keys.shape[0]
    new_dev = key_inputs.shape[0]
    n_dp = lax.axis_size("dp")
    n_q = lax.axis_size("queue")
    q = lax.axis_index("queue")
    dp = lax.axis_index("dp")
    piece_rows = k_dev // n_dp
    far_rows = (n_q - 1) * piece_rows

    fresh = jnp.dot(key_inputs, key_weight, preferred_element_type=jnp.float32)
    fresh = (fresh * lax.rsqrt(jnp.sum(fresh * fresh, -1, keepdims=True) + 1e-06)).astype(
        jnp.bfloat16
    )
    remote = gather_queue(queue_keys, n_q, n_dp)
    rows0 = far_rows

    query = jnp.dot(query_inputs, query_weight, preferred_element_type=jnp.float32)
    inv_len = lax.rsqrt(jnp.sum(query * query, -1, keepdims=True) + 1e-06)
    unit_f = query * inv_len
    unit = unit_f.astype(jnp.bfloat16)

    dims = (((1,), (1,)), ((), ()))
    near = lax.dot_general(unit, queue_keys, dims, preferred_element_type=jnp.float32) / temper
    far = lax.dot_general(unit, remote, dims, preferred_element_type=jnp.float32) / temper
    top = jnp.maximum(jnp.max(near, -1), jnp.max(far, -1))
    e_near = jnp.exp(near - top[:, None])
    e_far = jnp.exp(far - top[:, None])
    total = jnp.sum(e_near, -1) + jnp.sum(e_far, -1)
    mixture = jnp.dot(
        e_near.astype(jnp.bfloat16), queue_keys, preferred_element_type=jnp.float32
    ) + jnp.dot(e_far.astype(jnp.bfloat16), remote, preferred_element_type=jnp.float32)

    j = positive_index
    q_src = j // k_dev
    within = j % k_dev
    local = q_src == q
    e = dp ^ (within // piece_rows)
    s = (q - q_src) % n_q
    far_at = e * rows0 + (s - 1) * piece_rows + within % piece_rows
    pick_near = (local[:, None] & (within[:, None] == jnp.arange(k_dev)[None, :])).astype(
        jnp.bfloat16
    )
    pick_far = (
        (~local)[:, None] & (far_at[:, None] == jnp.arange(n_dp * rows0)[None, :])
    ).astype(jnp.bfloat16)
    chosen = jnp.dot(pick_near, queue_keys, preferred_element_type=jnp.float32) + jnp.dot(
        pick_far, remote, preferred_element_type=jnp.float32
    )

    mixture = mixture / total[:, None]
    positive = jnp.sum(unit.astype(jnp.float32) * chosen, -1) / temper
    loss = top + jnp.log(total) - positive
    grad_unit = (mixture - chosen) / temper
    grad_query = (
        (grad_unit - unit_f * jnp.sum(unit_f * grad_unit, -1, keepdims=True)) * inv_len
    ).astype(jnp.bfloat16)
    fresh, grad_query = lax.optimization_barrier((fresh, grad_query))
    along = blocks_over_queue(fresh, n_q)
    grad_rows, along = reduce_scatter_grad(query_inputs, grad_query, n_q, n_dp, along)
    blocks = gather_blocks(along, n_q, n_dp)

    n_blocks = slot_owner.shape[0]
    slots_here = q * n_dp + jnp.arange(n_dp, dtype=jnp.int32)
    match = slot_owner[None, :] == slots_here[:, None]
    owner_block = jnp.sum(jnp.where(match, jnp.arange(n_blocks, dtype=jnp.int32)[None, :], 0), -1)
    offset = (jnp.arange(k_dev, dtype=jnp.int32) - write_pointer[0]) % k_dev
    live = offset < n_dp * new_dev
    sub_block = jnp.minimum(offset // new_dev, n_dp - 1)
    b = jnp.take(owner_block, sub_block)
    b_e = dp ^ (b % n_dp)
    b_s = (q - b // n_dp) % n_q
    source = (b_e * n_q + b_s) * new_dev + offset % new_dev
    pick_new = (source[:, None] == jnp.arange(blocks.shape[0])[None, :]).astype(jnp.bfloat16)
    placed = jnp.dot(pick_new, blocks, preferred_element_type=jnp.float32).astype(jnp.bfloat16)
    new_queue = jnp.where(live[:, None], placed, queue_keys)
    return (loss, grad_rows, new_queue)


def solution(mesh):
    in_specs = (
        P(("groups", "queue", "dp"), None),
        P(("groups", "queue", "dp"), None),
        P(),
        P(),
        P(("groups", "queue"), None),
        P("groups"),
        P("groups"),
        P(("groups", "queue", "dp")),
    )
    out_specs = (
        P(("groups", "queue", "dp")),
        P(("groups", "queue", "dp"), None),
        P(("groups", "queue"), None),
    )
    return jax.shard_map(body, mesh=mesh, in_specs=in_specs, out_specs=out_specs, check_vma=False)
```

```python
import jax
import jax.numpy as jnp
from jax import lax
from jax.sharding import PartitionSpec as P

temper = 0.05


def shift(x, axis, n, step):
    return lax.ppermute(x, axis, [(i, (i + step) % n) for i in range(n)])


def swap(x, axis, n, bit):
    return lax.ppermute(x, axis, [(i, i ^ bit) for i in range(n)])


def dp_bits(n_dp):
    bits = []
    b = n_dp // 2
    while b >= 1:
        bits.append(b)
        b //= 2
    return bits


def gather_queue(queue_keys, n_q, n_dp):
    dp = lax.axis_index("dp")
    k_dev, width = queue_keys.shape
    piece_rows = k_dev // n_dp
    piece = lax.dynamic_slice_in_dim(queue_keys, dp * piece_rows, piece_rows, 0)
    payload = jnp.stack([shift(piece, "queue", n_q, s) for s in range(1, n_q)])
    for bit in dp_bits(n_dp):
        payload = jnp.stack([payload, swap(payload, "dp", n_dp, bit)], axis=0)
    return payload.reshape(-1, width)


def reversed_bits(m, n_dp):
    bits = dp_bits(n_dp)
    r = jnp.zeros_like(m)
    for t, bit in enumerate(bits):
        r = r + ((m // bit) % 2) * (1 << t)
    return r


def blocks_over_queue(block, n_q):
    return jnp.stack([block] + [shift(block, "queue", n_q, s) for s in range(1, n_q)])


def gather_blocks(got, n_q, n_dp):
    block = got[0]
    for t, bit in enumerate(dp_bits(n_dp)):
        got = jnp.stack([got, swap(got, "dp", n_dp, bit)], axis=t)
    return got.reshape(n_dp * n_q * block.shape[0], block.shape[1])


def reduce_scatter_grad(query_inputs, grad_query, n_q, n_dp, held):
    q = lax.axis_index("queue")
    dp = lax.axis_index("dp")
    q_dev, rows = query_inputs.shape
    width = grad_query.shape[1]
    share = rows // (n_q * n_dp)
    bits = dp_bits(n_dp)
    hb = bits[0]
    side = dp // hb
    x4 = query_inputs.reshape(q_dev, n_q, 2, hb * share)
    mine = lax.dynamic_index_in_dim(x4, side, 2, keepdims=False)
    other = lax.dynamic_index_in_dim(x4, 1 - side, 2, keepdims=False)
    got_x = swap(other, "dp", n_dp, hb)
    xs = jnp.concatenate([mine, got_x], axis=0).reshape(2 * q_dev, n_q * hb * share)
    rest = bits[1:]
    halves = 2
    cols = width // halves
    out = []
    for h in range(halves):
        g_h = grad_query[:, h * cols:(h + 1) * cols]
        got_g = swap(g_h, "dp", n_dp, hb)
        if h == halves - 1:
            held, got_g = lax.optimization_barrier((held, got_g))
        gs = jnp.concatenate([g_h, got_g], axis=0)
        term = lax.dot_general(xs, gs, (((0,), (0,)), ((), ())), preferred_element_type=jnp.float32)
        t = term.reshape((n_q,) + (2,) * len(rest) + (share, cols))
        for axis in reversed(range(len(rest))):
            bit = rest[axis]
            me = (dp // bit) % 2
            keep = lax.dynamic_index_in_dim(t, me, 1 + axis, keepdims=False)
            send = lax.dynamic_index_in_dim(t, 1 - me, 1 + axis, keepdims=False)
            t = keep + swap(send, "dp", n_dp, bit)
        t = t.reshape(n_q, share, cols)
        acc = lax.dynamic_index_in_dim(t, q, 0, keepdims=False)
        for s in range(1, n_q):
            part = lax.dynamic_index_in_dim(t, (q + s) % n_q, 0, keepdims=False)
            acc = acc + shift(part, "queue", n_q, s)
        out.append(acc)
    return jnp.concatenate(out, axis=1), held


def body(
    query_inputs,
    key_inputs,
    query_weight,
    key_weight,
    queue_keys,
    write_pointer,
    slot_owner,
    positive_index,
):
    q_dev, width = query_inputs.shape
    k_dev = queue_keys.shape[0]
    new_dev = key_inputs.shape[0]
    n_dp = lax.axis_size("dp")
    n_q = lax.axis_size("queue")
    q = lax.axis_index("queue")
    dp = lax.axis_index("dp")
    piece_rows = k_dev // n_dp
    far_rows = (n_q - 1) * piece_rows

    fresh = jnp.dot(key_inputs, key_weight, preferred_element_type=jnp.float32)
    fresh = (fresh * lax.rsqrt(jnp.sum(fresh * fresh, -1, keepdims=True) + 1e-06)).astype(
        jnp.bfloat16
    )
    remote = gather_queue(queue_keys, n_q, n_dp)
    rows0 = far_rows

    query = jnp.dot(query_inputs, query_weight, preferred_element_type=jnp.float32)
    inv_len = lax.rsqrt(jnp.sum(query * query, -1, keepdims=True) + 1e-06)
    unit_f = query * inv_len
    unit = unit_f.astype(jnp.bfloat16)

    dims = (((1,), (1,)), ((), ()))
    near = lax.dot_general(unit, queue_keys, dims, preferred_element_type=jnp.float32) / temper
    far = lax.dot_general(unit, remote, dims, preferred_element_type=jnp.float32) / temper
    top = jnp.maximum(jnp.max(near, -1), jnp.max(far, -1))
    e_near = jnp.exp(near - top[:, None])
    e_far = jnp.exp(far - top[:, None])
    total = jnp.sum(e_near, -1) + jnp.sum(e_far, -1)
    mixture = jnp.dot(
        e_near.astype(jnp.bfloat16), queue_keys, preferred_element_type=jnp.float32
    ) + jnp.dot(e_far.astype(jnp.bfloat16), remote, preferred_element_type=jnp.float32)

    j = positive_index
    q_src = j // k_dev
    within = j % k_dev
    local = q_src == q
    e = reversed_bits(dp ^ (within // piece_rows), n_dp)
    s = (q - q_src) % n_q
    far_at = e * rows0 + (s - 1) * piece_rows + within % piece_rows
    pick_near = (local[:, None] & (within[:, None] == jnp.arange(k_dev)[None, :])).astype(
        jnp.bfloat16
    )
    pick_far = (
        (~local)[:, None] & (far_at[:, None] == jnp.arange(n_dp * rows0)[None, :])
    ).astype(jnp.bfloat16)
    chosen = jnp.dot(pick_near, queue_keys, preferred_element_type=jnp.float32) + jnp.dot(
        pick_far, remote, preferred_element_type=jnp.float32
    )

    mixture = mixture / total[:, None]
    positive = jnp.sum(unit.astype(jnp.float32) * chosen, -1) / temper
    loss = top + jnp.log(total) - positive
    grad_unit = (mixture - chosen) / temper
    grad_query = (
        (grad_unit - unit_f * jnp.sum(unit_f * grad_unit, -1, keepdims=True)) * inv_len
    ).astype(jnp.bfloat16)
    fresh, grad_query = lax.optimization_barrier((fresh, grad_query))
    along = blocks_over_queue(fresh, n_q)
    grad_rows, along = reduce_scatter_grad(query_inputs, grad_query, n_q, n_dp, along)
    blocks = gather_blocks(along, n_q, n_dp)

    n_blocks = slot_owner.shape[0]
    slots_here = q * n_dp + jnp.arange(n_dp, dtype=jnp.int32)
    match = slot_owner[None, :] == slots_here[:, None]
    owner_block = jnp.sum(jnp.where(match, jnp.arange(n_blocks, dtype=jnp.int32)[None, :], 0), -1)
    offset = (jnp.arange(k_dev, dtype=jnp.int32) - write_pointer[0]) % k_dev
    live = offset < n_dp * new_dev
    sub_block = jnp.minimum(offset // new_dev, n_dp - 1)
    b = jnp.take(owner_block, sub_block)
    b_e = dp ^ (b % n_dp)
    b_s = (q - b // n_dp) % n_q
    source = (b_e * n_q + b_s) * new_dev + offset % new_dev
    pick_new = (source[:, None] == jnp.arange(blocks.shape[0])[None, :]).astype(jnp.bfloat16)
    placed = jnp.dot(pick_new, blocks, preferred_element_type=jnp.float32).astype(jnp.bfloat16)
    new_queue = jnp.where(live[:, None], placed, queue_keys)
    return (loss, grad_rows, new_queue)


def solution(mesh):
    in_specs = (
        P(("groups", "queue", "dp"), None),
        P(("groups", "queue", "dp"), None),
        P(),
        P(),
        P(("groups", "queue"), None),
        P("groups"),
        P("groups"),
        P(("groups", "queue", "dp")),
    )
    out_specs = (
        P(("groups", "queue", "dp")),
        P(("groups", "queue", "dp"), None),
        P(("groups", "queue"), None),
    )
    return jax.shard_map(body, mesh=mesh, in_specs=in_specs, out_specs=out_specs, check_vma=False)
```

```python
import jax
import jax.numpy as jnp
from jax import lax
from jax.sharding import PartitionSpec as P

temper = 0.05


def shift(x, axis, n, step):
    return lax.ppermute(x, axis, [(i, (i + step) % n) for i in range(n)])


def swap(x, axis, n, bit):
    return lax.ppermute(x, axis, [(i, i ^ bit) for i in range(n)])


def dp_bits(n_dp):
    bits = []
    b = n_dp // 2
    while b >= 1:
        bits.append(b)
        b //= 2
    return bits


def gather_queue(queue_keys, n_q, n_dp):
    dp = lax.axis_index("dp")
    k_dev, width = queue_keys.shape
    piece_rows = k_dev // n_dp
    piece = lax.dynamic_slice_in_dim(queue_keys, dp * piece_rows, piece_rows, 0)
    payload = jnp.stack([shift(piece, "queue", n_q, s) for s in range(1, n_q)])
    for t, bit in enumerate(dp_bits(n_dp)):
        payload = jnp.stack([payload, swap(payload, "dp", n_dp, bit)], axis=t)
    return payload.reshape(-1, width)


def blocks_over_queue(block, n_q):
    return jnp.stack([block] + [shift(block, "queue", n_q, s) for s in range(1, n_q)])


def gather_blocks(got, n_q, n_dp):
    block = got[0]
    for t, bit in enumerate(dp_bits(n_dp)):
        got = jnp.stack([got, swap(got, "dp", n_dp, bit)], axis=t)
    return got.reshape(n_dp * n_q * block.shape[0], block.shape[1])


def reduce_scatter_grad(query_inputs, grad_query, n_q, n_dp, held):
    q = lax.axis_index("queue")
    dp = lax.axis_index("dp")
    q_dev, rows = query_inputs.shape
    width = grad_query.shape[1]
    share = rows // (n_q * n_dp)
    bits = dp_bits(n_dp)
    hb = bits[0]
    side = dp // hb
    x4 = query_inputs.reshape(q_dev, n_q, 2, hb * share)
    mine = lax.dynamic_index_in_dim(x4, side, 2, keepdims=False)
    other = lax.dynamic_index_in_dim(x4, 1 - side, 2, keepdims=False)
    got_x = swap(other, "dp", n_dp, hb)
    x_mine = mine.reshape(q_dev, n_q * hb * share)
    x_got = got_x.reshape(q_dev, n_q * hb * share)
    tdims = (((0,), (0,)), ((), ()))
    rest = bits[1:]
    halves = 2
    cols = width // halves
    out = []
    for h in range(halves):
        g_h = grad_query[:, h * cols:(h + 1) * cols]
        got_g = swap(g_h, "dp", n_dp, hb)
        if h == halves - 1:
            held, got_g = lax.optimization_barrier((held, got_g))
        term = lax.dot_general(
            x_mine, g_h, tdims, preferred_element_type=jnp.float32
        ) + lax.dot_general(x_got, got_g, tdims, preferred_element_type=jnp.float32)
        t = term.reshape((n_q,) + (2,) * len(rest) + (share, cols))
        for axis in reversed(range(len(rest))):
            bit = rest[axis]
            me = (dp // bit) % 2
            keep = lax.dynamic_index_in_dim(t, me, 1 + axis, keepdims=False)
            send = lax.dynamic_index_in_dim(t, 1 - me, 1 + axis, keepdims=False)
            t = keep + swap(send, "dp", n_dp, bit)
        t = t.reshape(n_q, share, cols)
        acc = lax.dynamic_index_in_dim(t, q, 0, keepdims=False)
        for s in range(1, n_q):
            part = lax.dynamic_index_in_dim(t, (q + s) % n_q, 0, keepdims=False)
            acc = acc + shift(part, "queue", n_q, s)
        out.append(acc)
    return jnp.concatenate(out, axis=1), held


def body(
    query_inputs,
    key_inputs,
    query_weight,
    key_weight,
    queue_keys,
    write_pointer,
    slot_owner,
    positive_index,
):
    q_dev, width = query_inputs.shape
    k_dev = queue_keys.shape[0]
    new_dev = key_inputs.shape[0]
    n_dp = lax.axis_size("dp")
    n_q = lax.axis_size("queue")
    q = lax.axis_index("queue")
    dp = lax.axis_index("dp")
    piece_rows = k_dev // n_dp
    far_rows = (n_q - 1) * piece_rows

    fresh = jnp.dot(key_inputs, key_weight, preferred_element_type=jnp.float32)
    fresh = (fresh * lax.rsqrt(jnp.sum(fresh * fresh, -1, keepdims=True) + 1e-06)).astype(
        jnp.bfloat16
    )
    remote = gather_queue(queue_keys, n_q, n_dp)
    rows0 = far_rows

    query = jnp.dot(query_inputs, query_weight, preferred_element_type=jnp.float32)
    inv_len = lax.rsqrt(jnp.sum(query * query, -1, keepdims=True) + 1e-06)
    unit_f = query * inv_len
    unit = unit_f.astype(jnp.bfloat16)

    dims = (((1,), (1,)), ((), ()))
    near = lax.dot_general(unit, queue_keys, dims, preferred_element_type=jnp.float32) / temper
    far = lax.dot_general(unit, remote, dims, preferred_element_type=jnp.float32) / temper
    top = jnp.maximum(jnp.max(near, -1), jnp.max(far, -1))
    e_near = jnp.exp(near - top[:, None])
    e_far = jnp.exp(far - top[:, None])
    total = jnp.sum(e_near, -1) + jnp.sum(e_far, -1)
    mixture = jnp.dot(
        e_near.astype(jnp.bfloat16), queue_keys, preferred_element_type=jnp.float32
    ) + jnp.dot(e_far.astype(jnp.bfloat16), remote, preferred_element_type=jnp.float32)

    j = positive_index
    q_src = j // k_dev
    within = j % k_dev
    local = q_src == q
    e = dp ^ (within // piece_rows)
    s = (q - q_src) % n_q
    far_at = e * rows0 + (s - 1) * piece_rows + within % piece_rows
    pick_near = (local[:, None] & (within[:, None] == jnp.arange(k_dev)[None, :])).astype(
        jnp.bfloat16
    )
    pick_far = (
        (~local)[:, None] & (far_at[:, None] == jnp.arange(n_dp * rows0)[None, :])
    ).astype(jnp.bfloat16)
    chosen = jnp.dot(pick_near, queue_keys, preferred_element_type=jnp.float32) + jnp.dot(
        pick_far, remote, preferred_element_type=jnp.float32
    )

    mixture = mixture / total[:, None]
    positive = jnp.sum(unit.astype(jnp.float32) * chosen, -1) / temper
    loss = top + jnp.log(total) - positive
    grad_unit = (mixture - chosen) / temper
    grad_query = (
        (grad_unit - unit_f * jnp.sum(unit_f * grad_unit, -1, keepdims=True)) * inv_len
    ).astype(jnp.bfloat16)
    fresh, grad_query = lax.optimization_barrier((fresh, grad_query))
    along = blocks_over_queue(fresh, n_q)
    grad_rows, along = reduce_scatter_grad(query_inputs, grad_query, n_q, n_dp, along)
    blocks = gather_blocks(along, n_q, n_dp)

    n_blocks = slot_owner.shape[0]
    slots_here = q * n_dp + jnp.arange(n_dp, dtype=jnp.int32)
    match = slot_owner[None, :] == slots_here[:, None]
    owner_block = jnp.sum(jnp.where(match, jnp.arange(n_blocks, dtype=jnp.int32)[None, :], 0), -1)
    offset = (jnp.arange(k_dev, dtype=jnp.int32) - write_pointer[0]) % k_dev
    live = offset < n_dp * new_dev
    sub_block = jnp.minimum(offset // new_dev, n_dp - 1)
    b = jnp.take(owner_block, sub_block)
    b_e = dp ^ (b % n_dp)
    b_s = (q - b // n_dp) % n_q
    source = (b_e * n_q + b_s) * new_dev + offset % new_dev
    pick_new = (source[:, None] == jnp.arange(blocks.shape[0])[None, :]).astype(jnp.bfloat16)
    placed = jnp.dot(pick_new, blocks, preferred_element_type=jnp.float32).astype(jnp.bfloat16)
    new_queue = jnp.where(live[:, None], placed, queue_keys)
    return (loss, grad_rows, new_queue)


def solution(mesh):
    in_specs = (
        P(("groups", "queue", "dp"), None),
        P(("groups", "queue", "dp"), None),
        P(),
        P(),
        P(("groups", "queue"), None),
        P("groups"),
        P("groups"),
        P(("groups", "queue", "dp")),
    )
    out_specs = (
        P(("groups", "queue", "dp")),
        P(("groups", "queue", "dp"), None),
        P(("groups", "queue"), None),
    )
    return jax.shard_map(body, mesh=mesh, in_specs=in_specs, out_specs=out_specs, check_vma=False)
```
